128 devices in a mesh: mode: 8 (over x, core), member: 16 (over z, y).
Axes of the slice: x: 4, y: 4, z: 4, core: 2. Of those that a mesh axis runs over, the one named last changes fastest.
Arguments:
- ground_accel: bfloat16 [4, 639], replicated, may hold values from -6 to 6
- modal_kernel: bfloat16 [4096, 512], P(('mode', 'member')), may hold values from -0.25 to 0.25
- mode_shapes: bfloat16 [98304, 4096], P('member', 'mode'), may hold values from -0.09375 to 0.09375
- member_owner: int32 [16384, 1], P('member'), may hold values from 0 to 127; in each aligned block of 128 rows (0 to 127, 128 to 255, ...) at most 2 rows name the same one
- member_group: int32 [16384, 1], P('member'), may hold values from 0 to 3
- record_table: int32 [512, 8], P(('mode', 'member')), may hold values from 0 to 3
- case_coef: float32 [8, 6], replicated, may hold values from -1.5 to 1.5
- gravity: float32 [512, 8], P(('mode', 'member')), may hold values from -10 to 10
Outputs:
- demand: float32 [512, 8], P(('mode', 'member'))
The draws below stay inside these ranges and needn't reach their ends.
Inputs may be any that keep to these rules, and one draw needn't show every extreme that they name: `member_owner`: in each aligned block of 1024 / 8 members no owner is named more than 2 times, a bound that some block reaches.
All inputs are finite; a program needn't handle non-finite values.
Results may differ from the reference program's by a relative error of at most 0.0065.
Values may be sent and summed in bfloat16 or wider, within the bound.
No kernel may reach another device: no remote copies, remote signals or barrier semaphores. Data moves between devices by JAX's collectives and lax.ppermute only.
A program may use at most 64 MiB of HBM per device.

```python
import math
import jax
import jax.numpy as jnp
import numpy as np
from jax import lax

MODES = 4096
TAPS = 512
COMPS = 6
RECORDS = 4
CASES = 8
TW = 128
MEM_DEV = 1024
GROUP_DEV = 4
CAP = 2
SPAN = 639
MEMBERS = 16384
GROUPS = 512
N_MODE = 8
N_MEMBER = 16


def plant(array, stream_key, low, high):
    longest = array.shape.index(max(array.shape))
    spots = []
    for shift in (0, 1):
        where = [jax.random.randint(jax.random.fold_in(stream_key, axis), (), 0, length) for axis, length in enumerate(array.shape)]
        where[longest] = (where[longest] + shift) % array.shape[longest]
        spots.append(tuple(where))
    return array.at[spots[0]].set(low).at[spots[1]].set(high)


def block_levels(key, shape, shards, low, largest):
    gain = 1.0
    for position, shards_of in shards:
        steps = jax.random.uniform(jax.random.fold_in(jax.random.fold_in(key, 6), position), (shards_of,), jnp.float32, low / len(shards), largest / len(shards))
        gain = gain * jnp.repeat(jnp.exp(steps), shape[position] // shards_of).reshape((-1,) + (1,) * (len(shape) - 1 - position))
    return gain


def deal_out(key, own, number, rows, count, top, most, skew):
    ranking = jax.random.permutation(key, count)
    packed, common = portions_of(count, rows * top, most, skew, True), portions_of(count, rows * top, most, skew, False)
    places = jnp.arange(count)

    def named(sizes, rotation):
        used = int((sizes > 0).sum())
        fixed = max(1, used // 4)
        shifted = fixed + (places - fixed + rotation * (used - fixed)) % max(1, count - fixed)
        return jnp.zeros((count,), jnp.int32).at[ranking[jnp.where(places < fixed, places, shifted)]].set(jnp.asarray(sizes, jnp.int32))

    sizes = jnp.where(number % 4 == 0, named(packed, number // 4), named(common, number - number // 4 - 1))
    mixed = jax.random.permutation(jax.random.fold_in(own, 3), count)
    source_of, taker = mixed[0:count // 2 * 2:2], mixed[1:count // 2 * 2:2]
    margin = jnp.minimum(sizes[source_of] - 1, most - sizes[taker]) // 2
    margin = jnp.where((source_of == ranking[0]) | (taker == ranking[0]) | (sizes[taker] == 0), 0, jnp.maximum(margin, 0))
    shifted = jax.random.randint(jax.random.fold_in(own, 4), (count // 2,), 0, 1 << 20) % (margin + 1)
    sizes = sizes.at[source_of].add(-shifted).at[taker].add(shifted)
    members = jnp.searchsorted(jnp.cumsum(sizes), jnp.arange(rows * top), side="right").astype(jnp.int32)
    listing = members.reshape(top, rows).T
    listing = listing[jax.random.permutation(jax.random.fold_in(own, 1), rows)]
    rotation = jax.random.randint(jax.random.fold_in(own, 2), (rows, 1), 0, top)
    return jnp.take_along_axis(listing, (jnp.arange(top)[None, :] + rotation) % top, axis=1)


def portions_of(amount, total, limit, lean, full):
    loads = [(1 << 20) // math.isqrt(rank ** lean) + 1 for rank in range(1, amount + 1)]
    largest = limit if full else min(limit, max(-(-total // amount), total * loads[0] // sum(loads)))
    least = 1 if total - largest >= amount - 1 else 0
    counts, spare = [largest] + [least] * (amount - 1), total - largest - least * (amount - 1)
    while spare > 0:
        free = [i for i in range(1, amount) if counts[i] < largest] or [i for i in range(1, amount) if counts[i] < limit]
        mass, budget = sum([loads[i] for i in free]), spare
        for i in free:
            addition = min(limit - counts[i], max(1, budget * loads[i] // mass), spare)
            counts[i] = counts[i] + addition
            spare = spare - addition
    return np.array(counts)


def centred(stream_key, dims, scale, bound, cuts=(), kind=jnp.bfloat16):
    loudness = block_levels(stream_key, dims, cuts, -0.22, 0.18) if cuts else 1.0
    drawn = jax.random.normal(stream_key, dims, jnp.float32) * scale * loudness
    return jnp.minimum(jnp.maximum(drawn, -bound), bound).astype(kind)


def setup_inputs(seed: int = 0) -> dict:
    splits = jax.random.split(jax.random.key(seed), 9)
    ground_accel = centred(splits[0], (RECORDS, SPAN), 1.0, 6.0)
    modal_kernel = centred(splits[1], (MODES, TAPS), TAPS ** -0.5, 0.25, ((0, 128),))
    mode_shapes = centred(splits[2], (MEMBERS * COMPS, MODES), MODES ** -0.5, 0.09375, ((0, 16), (1, 8)))
    member_owner_keys = jax.random.split(jax.random.fold_in(splits[3], 1), MEMBERS // (MEM_DEV // N_MODE))
    member_owner_turns = jax.random.permutation(jax.random.fold_in(splits[3], 3), MEMBERS // (MEM_DEV // N_MODE))
    member_owner = jax.vmap(lambda own, number: deal_out(jax.random.fold_in(splits[3], 2), own, number, MEM_DEV // N_MODE, N_MODE * N_MEMBER, 1, CAP, 2))(member_owner_keys, member_owner_turns).reshape((MEMBERS, 1))
    member_group = plant(jax.random.randint(splits[4], (MEMBERS, 1), 0, GROUP_DEV), jax.random.fold_in(splits[4], 1), 0, GROUP_DEV - 1).astype(jnp.int32)
    record_table = plant(jax.random.randint(splits[5], (GROUPS, CASES), 0, RECORDS), jax.random.fold_in(splits[5], 1), 0, RECORDS - 1).astype(jnp.int32)
    case_coef = centred(splits[6], (CASES, COMPS), 0.3, 1.5, (), jnp.float32)
    gravity = centred(splits[7], (GROUPS, CASES), 2.0, 10.0, ((0, 128),), jnp.float32)
    return {"ground_accel": ground_accel, "modal_kernel": modal_kernel, "mode_shapes": mode_shapes, "member_owner": member_owner, "member_group": member_group, "record_table": record_table, "case_coef": case_coef, "gravity": gravity}


def reference(ground_accel, modal_kernel, mode_shapes, member_owner, member_group, record_table, case_coef, gravity):
    offsets = TAPS - 1 + jnp.arange(TW)[None, :] - jnp.arange(TAPS)[:, None]
    lagged = jnp.transpose(ground_accel[:, offsets], (1, 0, 2)).reshape(TAPS, RECORDS * TW)
    modal_resp = jnp.dot(modal_kernel, lagged, preferred_element_type=jnp.float32).astype(jnp.bfloat16)
    block_modes = MODES // N_MODE

    def add_block(running, block_index):
        first_mode = (block_index * block_modes).astype(jnp.int32)
        shapes = lax.dynamic_slice_in_dim(mode_shapes, first_mode, block_modes, 1)
        resp_rows = lax.dynamic_slice_in_dim(modal_resp, first_mode, block_modes, 0)
        partial_term = jnp.dot(shapes, resp_rows, preferred_element_type=jnp.float32).astype(jnp.bfloat16)
        partial_term = lax.optimization_barrier(partial_term)
        return running + partial_term.astype(jnp.float32), None

    start_total = jnp.zeros((MEMBERS * COMPS, RECORDS * TW), jnp.float32)
    forces = lax.scan(add_block, start_total, jnp.arange(N_MODE, dtype=jnp.int32))[0]
    group_index = (member_owner[:, 0] * GROUP_DEV + member_group[:, 0]).astype(jnp.int32)
    group_sums = jax.ops.segment_sum(forces.reshape(MEMBERS, COMPS * RECORDS * TW), group_index, num_segments=GROUPS)
    group_sums = group_sums.reshape(GROUPS, COMPS, RECORDS, TW)
    case_mix = jnp.einsum("sc,gcrt->gsrt", case_coef.astype(jnp.float32), group_sums, precision=lax.Precision.HIGHEST)
    record_pick = (record_table[:, :, None] == jnp.arange(RECORDS, dtype=jnp.int32)[None, None, :]).astype(jnp.float32)
    selected = jnp.sum(record_pick[:, :, :, None] * case_mix, axis=2)
    combined = gravity[:, :, None] + selected
    return jnp.max(jnp.abs(combined), axis=2)
```

```python
import jax
import jax.numpy as jnp
from jax import lax
from jax.sharding import PartitionSpec as P


def lagged_table(ground_accel, tap_count):
    record_count, span_len = ground_accel.shape
    step_count = span_len - tap_count + 1
    tiled = jnp.tile(ground_accel, (1, step_count + 1))[:, : step_count * (span_len + 1)]
    windows = tiled.reshape(record_count, step_count, span_len + 1)[:, :, :tap_count]
    return windows.reshape(record_count * step_count, tap_count)


def local(
    ground_accel,
    modal_kernel,
    mode_shapes,
    member_owner,
    member_group,
    record_table,
    case_coef,
    gravity,
):
    tap_count = modal_kernel.shape[1]
    record_count = ground_accel.shape[0]
    comp_count = case_coef.shape[1]
    group_count = gravity.shape[0]
    n_mode = lax.axis_size("mode")
    n_member = lax.axis_size("member")
    lagged = lagged_table(ground_accel, tap_count)
    local_resp = lax.dot_general(
        modal_kernel[:, ::-1], lagged, (((1,), (1,)), ((), ())), preferred_element_type=jnp.float32
    ).astype(jnp.bfloat16)
    modal_resp = lax.all_gather(local_resp, "member", axis=0, tiled=True)
    own_rows = mode_shapes.shape[0] // n_mode
    forces = lax.psum_scatter(
        jnp.dot(mode_shapes, modal_resp, preferred_element_type=jnp.float32).astype(jnp.bfloat16),
        "mode",
        scatter_dimension=0,
        tiled=True,
    ).astype(jnp.float32)
    members_here = own_rows // comp_count
    owner_total = n_mode * n_member
    slot_depth = max(2, 2 * members_here // owner_total)
    packed = forces.reshape(members_here, comp_count * forces.shape[1])
    first_row = lax.axis_index("mode") * members_here
    owner_ids = lax.dynamic_slice_in_dim(member_owner[:, 0], first_row, members_here)
    group_ids = lax.dynamic_slice_in_dim(member_group[:, 0], first_row, members_here)
    position = jnp.arange(members_here)
    earlier = (owner_ids[:, None] == owner_ids[None, :]) & (position[None, :] < position[:, None])
    member_rank = jnp.sum(earlier.astype(jnp.int32), axis=1)
    slot_index = owner_ids * slot_depth + member_rank
    slot_total = owner_total * slot_depth
    placement = jnp.arange(slot_total)[:, None] == slot_index[None, :]
    outgoing = jnp.dot(placement.astype(jnp.float32), packed, precision=lax.Precision.HIGHEST)
    slot_labels = jnp.max(jnp.where(placement, group_ids[None, :], -1), axis=1)
    incoming, slot_tags = (
        lax.all_to_all(
            outgoing.reshape(owner_total, slot_depth, -1).astype(jnp.bfloat16),
            ("mode", "member"),
            split_axis=0,
            concat_axis=0,
            tiled=True,
        ).astype(jnp.float32),
        lax.all_to_all(
            slot_labels.reshape(owner_total, slot_depth),
            ("mode", "member"),
            split_axis=0,
            concat_axis=0,
            tiled=True,
        ),
    )
    selector = (jnp.arange(group_count)[:, None] == slot_tags.reshape(-1)[None, :]).astype(
        jnp.float32
    )
    group_sums = jnp.dot(
        selector, incoming.reshape(selector.shape[1], -1), precision=lax.Precision.HIGHEST
    )
    group_sums = group_sums.reshape(group_count, comp_count, record_count, -1)
    case_mix = jnp.einsum("sc,gcrt->gsrt", case_coef, group_sums, precision=lax.Precision.HIGHEST)
    record_pick = (record_table[:, :, None] == jnp.arange(record_count)[None, None, :]).astype(
        jnp.float32
    )
    selected = jnp.sum(record_pick[:, :, :, None] * case_mix, axis=2)
    combined = gravity[:, :, None] + selected
    return jnp.max(jnp.abs(combined), axis=2)


def solution(mesh):
    placed = (
        P(),
        P(("mode", "member"), None),
        P("member", "mode"),
        P("member", None),
        P("member", None),
        P(("mode", "member"), None),
        P(),
        P(("mode", "member"), None),
    )
    return jax.shard_map(
        local, mesh=mesh, in_specs=placed, out_specs=P(("mode", "member"), None), check_vma=False
    )
```

```python
import jax
import jax.numpy as jnp
from jax import lax
from jax.sharding import PartitionSpec as P


def lagged_table(ground_accel, tap_count):
    record_count, span_len = ground_accel.shape
    step_count = span_len - tap_count + 1
    tiled = jnp.tile(ground_accel, (1, step_count + 1))[:, : step_count * (span_len + 1)]
    windows = tiled.reshape(record_count, step_count, span_len + 1)[:, :, :tap_count]
    return windows.reshape(record_count * step_count, tap_count)


def local(
    ground_accel,
    modal_kernel,
    mode_shapes,
    member_owner,
    member_group,
    record_table,
    case_coef,
    gravity,
):
    tap_count = modal_kernel.shape[1]
    record_count = ground_accel.shape[0]
    comp_count = case_coef.shape[1]
    n_mode = lax.axis_size("mode")
    n_member = lax.axis_size("member")
    groups_here = gravity.shape[0]
    group_total = groups_here * n_mode * n_member
    lagged = lagged_table(ground_accel, tap_count)
    local_resp = lax.dot_general(
        modal_kernel[:, ::-1], lagged, (((1,), (1,)), ((), ())), preferred_element_type=jnp.float32
    ).astype(jnp.bfloat16)
    modal_resp = lax.all_gather(local_resp, "member", axis=0, tiled=True)
    partial = jnp.dot(mode_shapes, modal_resp, preferred_element_type=jnp.float32).astype(
        jnp.bfloat16
    )
    members_here = member_owner.shape[0]
    packed = partial.reshape(members_here, comp_count * partial.shape[1])
    group_index = member_owner[:, 0] * groups_here + member_group[:, 0]
    selector = (jnp.arange(group_total)[:, None] == group_index[None, :]).astype(jnp.bfloat16)
    group_part = jnp.dot(selector, packed, preferred_element_type=jnp.float32)
    by_mode = lax.psum_scatter(
        group_part.astype(jnp.bfloat16), "mode", scatter_dimension=0, tiled=True
    )
    group_sums = lax.psum_scatter(
        by_mode.astype(jnp.float32), "member", scatter_dimension=0, tiled=True
    )
    group_sums = group_sums.reshape(groups_here, comp_count, record_count, -1)
    case_mix = jnp.einsum("sc,gcrt->gsrt", case_coef, group_sums, precision=lax.Precision.HIGHEST)
    record_pick = (record_table[:, :, None] == jnp.arange(record_count)[None, None, :]).astype(
        jnp.float32
    )
    selected = jnp.sum(record_pick[:, :, :, None] * case_mix, axis=2)
    combined = gravity[:, :, None] + selected
    return jnp.max(jnp.abs(combined), axis=2)


def solution(mesh):
    placed = (
        P(),
        P(("mode", "member"), None),
        P("member", "mode"),
        P("member", None),
        P("member", None),
        P(("mode", "member"), None),
        P(),
        P(("mode", "member"), None),
    )
    return jax.shard_map(
        local, mesh=mesh, in_specs=placed, out_specs=P(("mode", "member"), None), check_vma=False
    )
```

```python
import jax
import jax.numpy as jnp
from jax import lax
from jax.sharding import PartitionSpec as P


def lagged_table(ground_accel, tap_count):
    record_count, span_len = ground_accel.shape
    step_count = span_len - tap_count + 1
    tiled = jnp.tile(ground_accel, (1, step_count + 1))[:, : step_count * (span_len + 1)]
    windows = tiled.reshape(record_count, step_count, span_len + 1)[:, :, :tap_count]
    return windows.reshape(record_count * step_count, tap_count)


def local(
    ground_accel,
    modal_kernel,
    mode_shapes,
    member_owner,
    member_group,
    record_table,
    case_coef,
    gravity,
):
    tap_count = modal_kernel.shape[1]
    record_count = ground_accel.shape[0]
    comp_count = case_coef.shape[1]
    n_mode = lax.axis_size("mode")
    n_member = lax.axis_size("member")
    groups_here = gravity.shape[0]
    group_total = groups_here * n_mode * n_member
    lagged = lagged_table(ground_accel, tap_count)
    local_resp = lax.dot_general(
        modal_kernel[:, ::-1], lagged, (((1,), (1,)), ((), ())), preferred_element_type=jnp.float32
    ).astype(jnp.bfloat16)
    modal_resp = lax.all_gather(local_resp, "member", axis=0, tiled=True)
    partial = jnp.dot(mode_shapes, modal_resp, preferred_element_type=jnp.float32).astype(
        jnp.bfloat16
    )
    members_here = member_owner.shape[0]
    packed = partial.reshape(members_here, comp_count * partial.shape[1])
    group_index = member_owner[:, 0] * groups_here + member_group[:, 0]
    selector = (jnp.arange(group_total)[:, None] == group_index[None, :]).astype(jnp.bfloat16)
    group_part = jnp.dot(selector, packed, preferred_element_type=jnp.float32)
    group_part = group_part.reshape(group_total, comp_count, record_count, -1)
    all_records = lax.all_gather(record_table, ("mode", "member"), axis=0, tiled=True)
    record_pick = (all_records[:, :, None] == jnp.arange(record_count)[None, None, :]).astype(
        jnp.float32
    )
    case_mix = jnp.einsum("sc,gcrt->gsrt", case_coef, group_part, precision=lax.Precision.HIGHEST)
    share = jnp.sum(record_pick[:, :, :, None] * case_mix, axis=2)
    owner_total = n_mode * n_member
    share = share.reshape(owner_total, groups_here, share.shape[1], share.shape[2])
    received = lax.all_to_all(
        share.astype(jnp.bfloat16), ("mode", "member"), split_axis=0, concat_axis=0, tiled=True
    )
    selected = jnp.sum(received.astype(jnp.float32), axis=0)
    combined = gravity[:, :, None] + selected
    return jnp.max(jnp.abs(combined), axis=2)


def solution(mesh):
    placed = (
        P(),
        P(("mode", "member"), None),
        P("member", "mode"),
        P("member", None),
        P("member", None),
        P(("mode", "member"), None),
        P(),
        P(("mode", "member"), None),
    )
    return jax.shard_map(
        local, mesh=mesh, in_specs=placed, out_specs=P(("mode", "member"), None), check_vma=False
    )
```

```python
import functools

import jax
import jax.numpy as jnp
from jax import lax
from jax.experimental import pallas as pl
from jax.experimental.pallas import tpu as pltpu
from jax.sharding import PartitionSpec as P


def lagged_table(ground_accel, tap_count):
    record_count, span_len = ground_accel.shape
    step_count = span_len - tap_count + 1
    tiled = jnp.tile(ground_accel, (1, step_count + 1))[:, : step_count * (span_len + 1)]
    windows = tiled.reshape(record_count, step_count, span_len + 1)[:, :, :tap_count]
    return windows.reshape(record_count * step_count, tap_count)


def group_kernel(ms_ref, resp_ref, sel_ref, q_ref, p_scr, *, comps, tile):
    @pl.when(pl.program_id(0) == 0)
    def _():
        q_ref[...] = jnp.zeros_like(q_ref)

    part = jnp.dot(ms_ref[...], resp_ref[...], preferred_element_type=jnp.float32)
    part = part.astype(jnp.bfloat16).astype(jnp.float32)
    slabs = p_scr.shape[0]
    for k in range(slabs):
        p_scr[k] = part[:, k * 128 : (k + 1) * 128]
    sel = sel_ref[...]
    for c in range(comps):
        comp_rows = jnp.concatenate(
            [p_scr[k, pl.ds(c, tile, stride=comps), :] for k in range(slabs)], axis=1
        ).astype(jnp.bfloat16)
        q_ref[c] += jnp.dot(sel, comp_rows, preferred_element_type=jnp.float32)


def group_parts(mode_shapes, modal_resp, selector, comps, tile=128):
    modes = mode_shapes.shape[1]
    groups, members = selector.shape
    width = modal_resp.shape[1]
    return pl.pallas_call(
        functools.partial(group_kernel, comps=comps, tile=tile),
        grid=(members // tile,),
        in_specs=[
            pl.BlockSpec((tile * comps, modes), lambda k: (k, 0)),
            pl.BlockSpec((modes, width), lambda k: (0, 0)),
            pl.BlockSpec((groups, tile), lambda k: (0, k)),
        ],
        out_specs=pl.BlockSpec((comps, groups, width), lambda k: (0, 0, 0)),
        out_shape=jax.ShapeDtypeStruct((comps, groups, width), jnp.float32),
        scratch_shapes=[pltpu.VMEM((width // 128, tile * comps, 128), jnp.float32)],
        compiler_params=pltpu.CompilerParams(vmem_limit_bytes=48 * 1024 * 1024),
    )(mode_shapes, modal_resp, selector)


def local(
    ground_accel,
    modal_kernel,
    mode_shapes,
    member_owner,
    member_group,
    record_table,
    case_coef,
    gravity,
):
    tap_count = modal_kernel.shape[1]
    record_count = ground_accel.shape[0]
    comp_count = case_coef.shape[1]
    n_mode = lax.axis_size("mode")
    n_member = lax.axis_size("member")
    groups_here, case_count = gravity.shape
    owner_total = n_mode * n_member
    group_total = groups_here * owner_total
    lagged = lagged_table(ground_accel, tap_count)
    local_resp = lax.dot_general(
        modal_kernel[:, ::-1], lagged, (((1,), (1,)), ((), ())), preferred_element_type=jnp.float32
    ).astype(jnp.bfloat16)
    resp_rows, width = local_resp.shape
    rec_col = lax.all_gather(record_table, "mode", axis=0, tiled=True).reshape(-1)
    rec_rows = -(-rec_col.shape[0] // width)
    rec_rows = -(-rec_rows // 8) * 8
    rec_block = jnp.zeros((rec_rows * width,), jnp.bfloat16).at[: rec_col.shape[0]].set(
        rec_col.astype(jnp.bfloat16)
    )
    payload = jnp.concatenate([local_resp, rec_block.reshape(rec_rows, width)], axis=0)
    gathered = lax.all_gather(payload, "member", axis=0)
    modal_resp = gathered[:, :resp_rows].reshape(n_member * resp_rows, width)
    rec_all = gathered[:, resp_rows:].reshape(n_member, -1)[:, : rec_col.shape[0]]
    rec_all = rec_all.astype(jnp.int32).reshape(n_member, n_mode, groups_here, case_count)
    rec_all = jnp.transpose(rec_all, (1, 0, 2, 3)).reshape(group_total, case_count)

    group_index = member_owner[:, 0] * groups_here + member_group[:, 0]
    selector = (jnp.arange(group_total)[:, None] == group_index[None, :]).astype(jnp.bfloat16)
    group_part = group_parts(mode_shapes, modal_resp, selector, comp_count)
    group_part = group_part.reshape(comp_count, group_total, record_count, -1)
    record_pick = (rec_all[:, :, None] == jnp.arange(record_count)[None, None, :]).astype(
        jnp.float32
    )
    picked = jnp.sum(record_pick[None, :, :, :, None] * group_part[:, :, None, :, :], axis=3)
    share = jnp.sum(case_coef.T[:, None, :, None] * picked, axis=0)
    share = share.reshape(owner_total, groups_here, case_count, share.shape[-1])
    received = lax.all_to_all(
        share.astype(jnp.bfloat16), ("mode", "member"), split_axis=0, concat_axis=0, tiled=True
    )
    selected = jnp.sum(received.astype(jnp.float32), axis=0)
    combined = gravity[:, :, None] + selected
    return jnp.max(jnp.abs(combined), axis=2)


def solution(mesh):
    placed = (
        P(),
        P(("mode", "member"), None),
        P("member", "mode"),
        P("member", None),
        P("member", None),
        P(("mode", "member"), None),
        P(),
        P(("mode", "member"), None),
    )
    return jax.shard_map(
        local, mesh=mesh, in_specs=placed, out_specs=P(("mode", "member"), None), check_vma=False
    )
```

```python
import functools

import jax
import jax.numpy as jnp
from jax import lax
from jax.experimental import pallas as pl
from jax.experimental.pallas import tpu as pltpu
from jax.sharding import PartitionSpec as P


def lagged_table(ground_accel, tap_count):
    record_count, span_len = ground_accel.shape
    step_count = span_len - tap_count + 1
    tiled = jnp.tile(ground_accel, (1, step_count + 1))[:, : step_count * (span_len + 1)]
    windows = tiled.reshape(record_count, step_count, span_len + 1)[:, :, :tap_count]
    return windows.reshape(record_count * step_count, tap_count)


def group_kernel(
    coef_ref, ms_ref, resp_ref, sel_ref, pick_ref, out_ref, p_scr, q_scr, *, comps, tile, records
):
    k = pl.program_id(0)
    rows = tile * comps
    slabs, _, lanes = p_scr.shape
    part = jnp.dot(ms_ref[...], resp_ref[...], preferred_element_type=jnp.float32)
    part = part.astype(jnp.bfloat16).astype(jnp.float32)
    for l in range(slabs):
        p_scr[l, pl.ds(pl.multiple_of(k * rows, 8), rows), :] = part[:, l * lanes : (l + 1) * lanes]

    @pl.when(k == pl.num_programs(0) - 1)
    def _():
        sel = sel_ref[...]
        groups, members = sel.shape
        for c in range(comps):
            comp_rows = jnp.concatenate(
                [p_scr[l, pl.ds(c, members, stride=comps), :] for l in range(slabs)], axis=1
            ).astype(jnp.bfloat16)
            q_scr[c] = jnp.dot(sel, comp_rows, preferred_element_type=jnp.float32)
        cases = coef_ref.shape[0]
        steps = q_scr.shape[2] // records
        chunk = 64

        def mix(i, carry):
            g0 = pl.multiple_of(i * chunk, chunk)
            for s in range(cases):
                acc = jnp.zeros((chunk, steps), jnp.float32)
                for r in range(records):
                    mixed = coef_ref[s, 0] * q_scr[0, pl.ds(g0, chunk), pl.ds(r * steps, steps)]
                    for c in range(1, comps):
                        mixed = mixed + coef_ref[s, c] * q_scr[
                            c, pl.ds(g0, chunk), pl.ds(r * steps, steps)
                        ]
                    pick = pick_ref[pl.ds(g0, chunk), pl.ds(s * records + r, 1)]
                    acc = acc + pick * mixed
                out_ref[pl.ds(g0 * cases + s, chunk, stride=cases), :] = acc
            return carry

        lax.fori_loop(0, groups // chunk, mix, 0)


def group_shares(case_coef, mode_shapes, modal_resp, selector, record_pick, comps, tile=128):
    rows, modes = mode_shapes.shape
    groups, members = selector.shape
    width = modal_resp.shape[1]
    cases = case_coef.shape[0]
    records = record_pick.shape[1] // cases
    steps = width // records
    return pl.pallas_call(
        functools.partial(group_kernel, comps=comps, tile=tile, records=records),
        grid=(members // tile,),
        in_specs=[
            pl.BlockSpec(memory_space=pltpu.SMEM),
            pl.BlockSpec((tile * comps, modes), lambda k: (k, 0)),
            pl.BlockSpec((modes, width), lambda k: (0, 0)),
            pl.BlockSpec((groups, members), lambda k: (0, 0)),
            pl.BlockSpec((groups, cases * records), lambda k: (0, 0)),
        ],
        out_specs=pl.BlockSpec((groups * cases, steps), lambda k: (0, 0)),
        out_shape=jax.ShapeDtypeStruct((groups * cases, steps), jnp.float32),
        scratch_shapes=[
            pltpu.VMEM((width // 128, rows, 128), jnp.float32),
            pltpu.VMEM((comps, groups, width), jnp.float32),
        ],
        compiler_params=pltpu.CompilerParams(vmem_limit_bytes=56 * 1024 * 1024),
    )(case_coef, mode_shapes, modal_resp, selector, record_pick)


def local(
    ground_accel,
    modal_kernel,
    mode_shapes,
    member_owner,
    member_group,
    record_table,
    case_coef,
    gravity,
):
    tap_count = modal_kernel.shape[1]
    record_count = ground_accel.shape[0]
    comp_count = case_coef.shape[1]
    n_mode = lax.axis_size("mode")
    n_member = lax.axis_size("member")
    groups_here, case_count = gravity.shape
    owner_total = n_mode * n_member
    group_total = groups_here * owner_total
    lagged = lagged_table(ground_accel, tap_count)
    local_resp = lax.dot_general(
        modal_kernel[:, ::-1], lagged, (((1,), (1,)), ((), ())), preferred_element_type=jnp.float32
    ).astype(jnp.bfloat16)
    resp_rows, width = local_resp.shape
    rec_col = lax.all_gather(record_table, "mode", axis=0, tiled=True).reshape(-1)
    rec_rows = -(-rec_col.shape[0] // width)
    rec_rows = -(-rec_rows // 8) * 8
    rec_block = jnp.zeros((rec_rows * width,), jnp.bfloat16).at[: rec_col.shape[0]].set(
        rec_col.astype(jnp.bfloat16)
    )
    payload = jnp.concatenate([local_resp, rec_block.reshape(rec_rows, width)], axis=0)
    gathered = lax.all_gather(payload, "member", axis=0)
    modal_resp = gathered[:, :resp_rows].reshape(n_member * resp_rows, width)
    rec_all = gathered[:, resp_rows:].reshape(n_member, -1)[:, : rec_col.shape[0]]
    rec_all = rec_all.astype(jnp.int32).reshape(n_member, n_mode, groups_here, case_count)
    rec_all = jnp.transpose(rec_all, (1, 0, 2, 3)).reshape(group_total, case_count)

    group_index = member_owner[:, 0] * groups_here + member_group[:, 0]
    selector = (jnp.arange(group_total)[:, None] == group_index[None, :]).astype(jnp.bfloat16)
    record_pick = (rec_all[:, :, None] == jnp.arange(record_count)[None, None, :]).astype(
        jnp.float32
    )
    share = group_shares(
        case_coef, mode_shapes, modal_resp, selector, record_pick.reshape(group_total, -1), comp_count
    )
    share = share.reshape(owner_total, groups_here, case_count, share.shape[-1])
    received = lax.all_to_all(
        share.astype(jnp.bfloat16), ("mode", "member"), split_axis=0, concat_axis=0, tiled=True
    )
    selected = jnp.sum(received.astype(jnp.float32), axis=0)
    combined = gravity[:, :, None] + selected
    return jnp.max(jnp.abs(combined), axis=2)


def solution(mesh):
    placed = (
        P(),
        P(("mode", "member"), None),
        P("member", "mode"),
        P("member", None),
        P("member", None),
        P(("mode", "member"), None),
        P(),
        P(("mode", "member"), None),
    )
    return jax.shard_map(
        local, mesh=mesh, in_specs=placed, out_specs=P(("mode", "member"), None), check_vma=False
    )
```

```python
import functools

import jax
import jax.numpy as jnp
from jax import lax
from jax.experimental import pallas as pl
from jax.experimental.pallas import tpu as pltpu
from jax.sharding import PartitionSpec as P


def lagged_table(ground_accel, tap_count):
    record_count, span_len = ground_accel.shape
    step_count = span_len - tap_count + 1
    tiled = jnp.tile(ground_accel, (1, step_count + 1))[:, : step_count * (span_len + 1)]
    windows = tiled.reshape(record_count, step_count, span_len + 1)[:, :, :tap_count]
    return windows.reshape(record_count * step_count, tap_count)


def group_kernel(
    coef_ref, ms_ref, resp_ref, sel_ref, pick_ref, out_ref, p_scr, q_scr, *, comps, tile, records
):
    k = pl.program_id(0)
    rows = tile * comps
    slabs, _, lanes = p_scr.shape
    part = jnp.dot(ms_ref[...], resp_ref[...], preferred_element_type=jnp.float32)
    part = part.astype(jnp.bfloat16).astype(jnp.float32)
    for l in range(slabs):
        p_scr[l, pl.ds(pl.multiple_of(k * rows, 8), rows), :] = part[:, l * lanes : (l + 1) * lanes]

    @pl.when(k == pl.num_programs(0) - 1)
    def _():
        sel = sel_ref[...]
        groups, members = sel.shape
        for c in range(comps):
            comp_rows = jnp.concatenate(
                [p_scr[l, pl.ds(c, members, stride=comps), :] for l in range(slabs)], axis=1
            ).astype(jnp.bfloat16)
            q_scr[c] = jnp.dot(sel, comp_rows, preferred_element_type=jnp.float32)
        cases = coef_ref.shape[0]
        steps = q_scr.shape[2] // records
        chunk = 64

        def mix(i, carry):
            g0 = pl.multiple_of(i * chunk, chunk)
            for s in range(cases):
                acc = jnp.zeros((chunk, steps), jnp.float32)
                for r in range(records):
                    mixed = coef_ref[s, 0] * q_scr[0, pl.ds(g0, chunk), pl.ds(r * steps, steps)]
                    for c in range(1, comps):
                        mixed = mixed + coef_ref[s, c] * q_scr[
                            c, pl.ds(g0, chunk), pl.ds(r * steps, steps)
                        ]
                    pick = pick_ref[pl.ds(g0, chunk), pl.ds(s * records + r, 1)]
                    acc = acc + pick * mixed
                out_ref[pl.ds(g0 * cases + s, chunk, stride=cases), :] = acc
            return carry

        lax.fori_loop(0, groups // chunk, mix, 0)


def group_shares(case_coef, mode_shapes, modal_resp, selector, record_pick, comps, tile=128):
    rows, modes = mode_shapes.shape
    groups, members = selector.shape
    width = modal_resp.shape[1]
    cases = case_coef.shape[0]
    records = record_pick.shape[1] // cases
    steps = width // records
    return pl.pallas_call(
        functools.partial(group_kernel, comps=comps, tile=tile, records=records),
        grid=(members // tile,),
        in_specs=[
            pl.BlockSpec(memory_space=pltpu.SMEM),
            pl.BlockSpec((tile * comps, modes), lambda k: (k, 0)),
            pl.BlockSpec((modes, width), lambda k: (0, 0)),
            pl.BlockSpec((groups, members), lambda k: (0, 0)),
            pl.BlockSpec((groups, cases * records), lambda k: (0, 0)),
        ],
        out_specs=pl.BlockSpec((groups * cases, steps), lambda k: (0, 0)),
        out_shape=jax.ShapeDtypeStruct((groups * cases, steps), jnp.float32),
        scratch_shapes=[
            pltpu.VMEM((width // 128, rows, 128), jnp.float32),
            pltpu.VMEM((comps, groups, width), jnp.float32),
        ],
        compiler_params=pltpu.CompilerParams(vmem_limit_bytes=56 * 1024 * 1024),
    )(case_coef, mode_shapes, modal_resp, selector, record_pick)


def local(
    ground_accel,
    modal_kernel,
    mode_shapes,
    member_owner,
    member_group,
    record_table,
    case_coef,
    gravity,
):
    tap_count = modal_kernel.shape[1]
    record_count = ground_accel.shape[0]
    comp_count = case_coef.shape[1]
    n_mode = lax.axis_size("mode")
    n_member = lax.axis_size("member")
    groups_here, case_count = gravity.shape
    owner_total = n_mode * n_member
    group_total = groups_here * owner_total
    lagged = lagged_table(ground_accel, tap_count)
    local_resp = lax.dot_general(
        modal_kernel[:, ::-1], lagged, (((1,), (1,)), ((), ())), preferred_element_type=jnp.float32
    ).astype(jnp.bfloat16)
    resp_rows, width = local_resp.shape
    rec_col = lax.all_to_all(
        jnp.broadcast_to(record_table[None], (n_mode,) + record_table.shape), "mode", 0, 0
    ).reshape(-1)
    rec_rows = -(-rec_col.shape[0] // width)
    rec_rows = -(-rec_rows // 8) * 8
    rec_block = jnp.zeros((rec_rows * width,), jnp.bfloat16).at[: rec_col.shape[0]].set(
        rec_col.astype(jnp.bfloat16)
    )
    payload = jnp.concatenate([local_resp, rec_block.reshape(rec_rows, width)], axis=0)
    gathered = lax.all_to_all(
        jnp.broadcast_to(payload[None], (n_member,) + payload.shape), "member", 0, 0
    )
    modal_resp = gathered[:, :resp_rows].reshape(n_member * resp_rows, width)
    rec_all = gathered[:, resp_rows:].reshape(n_member, -1)[:, : rec_col.shape[0]]
    rec_all = rec_all.astype(jnp.int32).reshape(n_member, n_mode, groups_here, case_count)
    rec_all = jnp.transpose(rec_all, (1, 0, 2, 3)).reshape(group_total, case_count)

    group_index = member_owner[:, 0] * groups_here + member_group[:, 0]
    selector = (jnp.arange(group_total)[:, None] == group_index[None, :]).astype(jnp.bfloat16)
    record_pick = (rec_all[:, :, None] == jnp.arange(record_count)[None, None, :]).astype(
        jnp.float32
    )
    share = group_shares(
        case_coef, mode_shapes, modal_resp, selector, record_pick.reshape(group_total, -1), comp_count
    )
    share = share.reshape(owner_total, groups_here, case_count, share.shape[-1])
    received = lax.all_to_all(
        share.astype(jnp.bfloat16), ("mode", "member"), split_axis=0, concat_axis=0, tiled=True
    )
    selected = jnp.sum(received.astype(jnp.float32), axis=0)
    combined = gravity[:, :, None] + selected
    return jnp.max(jnp.abs(combined), axis=2)


def solution(mesh):
    placed = (
        P(),
        P(("mode", "member"), None),
        P("member", "mode"),
        P("member", None),
        P("member", None),
        P(("mode", "member"), None),
        P(),
        P(("mode", "member"), None),
    )
    return jax.shard_map(
        local, mesh=mesh, in_specs=placed, out_specs=P(("mode", "member"), None), check_vma=False
    )
```

```python
import functools

import jax
import jax.numpy as jnp
from jax import lax
from jax.experimental import pallas as pl
from jax.experimental.pallas import tpu as pltpu
from jax.sharding import PartitionSpec as P


def lagged_table(ground_accel, tap_count):
    record_count, span_len = ground_accel.shape
    step_count = span_len - tap_count + 1
    tiled = jnp.tile(ground_accel, (1, step_count + 1))[:, : step_count * (span_len + 1)]
    windows = tiled.reshape(record_count, step_count, span_len + 1)[:, :, :tap_count]
    return windows.reshape(record_count * step_count, tap_count)


def group_kernel(
    coef_ref, ms_ref, resp_ref, sel_ref, pick_ref, out_ref, p_scr, q_scr, *, comps, tile, records
):
    k = pl.program_id(0)
    rows = tile * comps
    slabs, _, lanes = p_scr.shape
    part = jnp.dot(ms_ref[...], resp_ref[...], preferred_element_type=jnp.float32)
    part = part.astype(jnp.bfloat16).astype(jnp.float32)
    for l in range(slabs):
        p_scr[l, pl.ds(pl.multiple_of(k * rows, 8), rows), :] = part[:, l * lanes : (l + 1) * lanes]

    @pl.when(k == pl.num_programs(0) - 1)
    def _():
        sel = sel_ref[...]
        groups, members = sel.shape
        for c in range(comps):
            comp_rows = jnp.concatenate(
                [p_scr[l, pl.ds(c, members, stride=comps), :] for l in range(slabs)], axis=1
            ).astype(jnp.bfloat16)
            q_scr[c] = jnp.dot(sel, comp_rows, preferred_element_type=jnp.float32)
        cases = coef_ref.shape[0]
        steps = q_scr.shape[2] // records
        per = lanes // steps
        chunk = 64
        lane = lax.broadcasted_iota(jnp.int32, (chunk, lanes), 1)

        def mix(i, carry):
            g0 = pl.multiple_of(i * chunk, chunk)
            for u in range(cases // per):
                packed = None
                for e in range(per):
                    s = u * per + e
                    acc = jnp.zeros((chunk, lanes), jnp.float32)
                    for l in range(slabs):
                        cols = pl.ds(l * lanes, lanes)
                        mixed = coef_ref[s, 0] * q_scr[0, pl.ds(g0, chunk), cols]
                        for c in range(1, comps):
                            mixed = mixed + coef_ref[s, c] * q_scr[c, pl.ds(g0, chunk), cols]
                        weight = pick_ref[pl.ds(g0, chunk), pl.ds(s * records + l * per, 1)]
                        weight = jnp.broadcast_to(weight, (chunk, lanes))
                        for j in range(1, per):
                            other = pick_ref[pl.ds(g0, chunk), pl.ds(s * records + l * per + j, 1)]
                            weight = jnp.where(lane >= j * steps, other, weight)
                        acc = acc + weight * mixed
                    total = acc
                    for j in range(1, per):
                        total = total + pltpu.roll(acc, j * steps, 1)
                    packed = total if packed is None else jnp.where(lane >= e * steps, total, packed)
                out_ref[pl.ds(g0 * (cases // per) + u, chunk, stride=cases // per), :] = packed
            return carry

        lax.fori_loop(0, groups // chunk, mix, 0)


def group_shares(case_coef, mode_shapes, modal_resp, selector, record_pick, comps, tile=128):
    rows, modes = mode_shapes.shape
    groups, members = selector.shape
    width = modal_resp.shape[1]
    cases = case_coef.shape[0]
    records = record_pick.shape[1] // cases
    steps = width // records
    per = 128 // steps
    return pl.pallas_call(
        functools.partial(group_kernel, comps=comps, tile=tile, records=records),
        grid=(members // tile,),
        in_specs=[
            pl.BlockSpec(memory_space=pltpu.SMEM),
            pl.BlockSpec((tile * comps, modes), lambda k: (k, 0)),
            pl.BlockSpec((modes, width), lambda k: (0, 0)),
            pl.BlockSpec((groups, members), lambda k: (0, 0)),
            pl.BlockSpec((groups, cases * records), lambda k: (0, 0)),
        ],
        out_specs=pl.BlockSpec((groups * cases // per, 128), lambda k: (0, 0)),
        out_shape=jax.ShapeDtypeStruct((groups * cases // per, 128), jnp.float32),
        scratch_shapes=[
            pltpu.VMEM((width // 128, rows, 128), jnp.float32),
            pltpu.VMEM((comps, groups, width), jnp.float32),
        ],
        compiler_params=pltpu.CompilerParams(vmem_limit_bytes=56 * 1024 * 1024),
    )(case_coef, mode_shapes, modal_resp, selector, record_pick)


def local(
    ground_accel,
    modal_kernel,
    mode_shapes,
    member_owner,
    member_group,
    record_table,
    case_coef,
    gravity,
):
    tap_count = modal_kernel.shape[1]
    record_count = ground_accel.shape[0]
    comp_count = case_coef.shape[1]
    n_mode = lax.axis_size("mode")
    n_member = lax.axis_size("member")
    groups_here, case_count = gravity.shape
    owner_total = n_mode * n_member
    group_total = groups_here * owner_total
    halves = 2
    lagged = lagged_table(ground_accel, tap_count)
    lagged = lagged.reshape(record_count, halves, -1, tap_count)
    lagged = jnp.transpose(lagged, (1, 0, 2, 3)).reshape(-1, tap_count)
    local_resp = lax.dot_general(
        modal_kernel[:, ::-1], lagged, (((1,), (1,)), ((), ())), preferred_element_type=jnp.float32
    ).astype(jnp.bfloat16)
    resp_rows, resp_cols = local_resp.shape
    width = resp_cols // halves
    rec_col = lax.all_to_all(
        jnp.broadcast_to(record_table[None], (n_mode,) + record_table.shape), "mode", 0, 0
    ).reshape(-1)
    rec_rows = -(-rec_col.shape[0] // width)
    rec_rows = -(-rec_rows // 8) * 8
    rec_block = jnp.zeros((rec_rows * width,), jnp.bfloat16).at[: rec_col.shape[0]].set(
        rec_col.astype(jnp.bfloat16)
    )
    group_index = member_owner[:, 0] * groups_here + member_group[:, 0]
    selector = (jnp.arange(group_total)[:, None] == group_index[None, :]).astype(jnp.bfloat16)
    demand = None
    record_pick = None
    for h in range(halves):
        payload = local_resp[:, h * width : (h + 1) * width]
        if h == 0:
            payload = jnp.concatenate([payload, rec_block.reshape(rec_rows, width)], axis=0)
        gathered = lax.all_to_all(
            jnp.broadcast_to(payload[None], (n_member,) + payload.shape), "member", 0, 0
        )
        modal_resp = gathered[:, :resp_rows].reshape(n_member * resp_rows, width)
        if h == 0:
            rec_all = gathered[:, resp_rows:].reshape(n_member, -1)[:, : rec_col.shape[0]]
            rec_all = rec_all.astype(jnp.int32).reshape(n_member, n_mode, groups_here, case_count)
            rec_all = jnp.transpose(rec_all, (1, 0, 2, 3)).reshape(group_total, case_count)
            record_pick = (rec_all[:, :, None] == jnp.arange(record_count)[None, None, :]).astype(
                jnp.float32
            )
            record_pick = record_pick.reshape(group_total, -1)
        share = group_shares(case_coef, mode_shapes, modal_resp, selector, record_pick, comp_count)
        share = share.reshape(owner_total, groups_here, -1, share.shape[-1])
        received = lax.all_to_all(
            share.astype(jnp.bfloat16), ("mode", "member"), split_axis=0, concat_axis=0, tiled=True
        )
        selected = jnp.sum(received.astype(jnp.float32), axis=0)
        selected = selected.reshape(groups_here, case_count, -1)
        peak = jnp.max(jnp.abs(gravity[:, :, None] + selected), axis=2)
        demand = peak if demand is None else jnp.maximum(demand, peak)
    return demand


def solution(mesh):
    placed = (
        P(),
        P(("mode", "member"), None),
        P("member", "mode"),
        P("member", None),
        P("member", None),
        P(("mode", "member"), None),
        P(),
        P(("mode", "member"), None),
    )
    return jax.shard_map(
        local, mesh=mesh, in_specs=placed, out_specs=P(("mode", "member"), None), check_vma=False
    )
```

```python
import functools

import jax
import jax.numpy as jnp
from jax import lax
from jax.experimental import pallas as pl
from jax.experimental.pallas import tpu as pltpu
from jax.sharding import PartitionSpec as P


def lagged_table(ground_accel, tap_count):
    record_count, span_len = ground_accel.shape
    step_count = span_len - tap_count + 1
    tiled = jnp.tile(ground_accel, (1, step_count + 1))[:, : step_count * (span_len + 1)]
    windows = tiled.reshape(record_count, step_count, span_len + 1)[:, :, :tap_count]
    return windows.reshape(record_count * step_count, tap_count)


def shape_sum_kernel(ms_ref, gi_ref, gs_ref, m_scr, *, comps, tile):
    k = pl.program_id(0)
    rows = tile * comps
    slabs, _, lanes = m_scr.shape
    block = ms_ref[...].astype(jnp.float32)
    for l in range(slabs):
        m_scr[l, pl.ds(pl.multiple_of(k * rows, 8), rows), :] = block[:, l * lanes : (l + 1) * lanes]

    @pl.when(k == pl.num_programs(0) - 1)
    def _():
        groups = gs_ref.shape[1]
        members = gi_ref.shape[1]
        sel = (lax.broadcasted_iota(jnp.int32, (groups, members), 0) == gi_ref[...]).astype(
            jnp.bfloat16
        )
        for c in range(comps):
            comp_rows = jnp.concatenate(
                [m_scr[l, pl.ds(c, members, stride=comps), :] for l in range(slabs)], axis=1
            ).astype(jnp.bfloat16)
            gs_ref[c] = jnp.dot(sel, comp_rows, preferred_element_type=jnp.float32).astype(
                jnp.bfloat16
            )


def shape_sums(mode_shapes, group_index, groups, comps, tile=128):
    rows, modes = mode_shapes.shape
    members = group_index.shape[1]
    return pl.pallas_call(
        functools.partial(shape_sum_kernel, comps=comps, tile=tile),
        grid=(members // tile,),
        in_specs=[
            pl.BlockSpec((tile * comps, modes), lambda k: (k, 0)),
            pl.BlockSpec((1, members), lambda k: (0, 0)),
        ],
        out_specs=pl.BlockSpec((comps, groups, modes), lambda k: (0, 0, 0)),
        out_shape=jax.ShapeDtypeStruct((comps, groups, modes), jnp.bfloat16),
        scratch_shapes=[pltpu.VMEM((modes // 128, rows, 128), jnp.float32)],
        compiler_params=pltpu.CompilerParams(vmem_limit_bytes=48 * 1024 * 1024),
    )(mode_shapes, group_index)


def mix_kernel(coef_ref, gs_ref, resp_ref, pick_ref, out_ref, q_scr, *, records):
    c = pl.program_id(0)
    comps = pl.num_programs(0)
    q_scr[c] = jnp.dot(gs_ref[0], resp_ref[...], preferred_element_type=jnp.float32)

    @pl.when(c == comps - 1)
    def _():
        groups = q_scr.shape[1]
        cases = coef_ref.shape[0]
        steps = q_scr.shape[2] // records
        chunk = 64

        def mix(i, carry):
            g0 = pl.multiple_of(i * chunk, chunk)
            for s in range(cases):
                acc = jnp.zeros((chunk, steps), jnp.float32)
                for r in range(records):
                    cols = pl.ds(r * steps, steps)
                    mixed = coef_ref[s, 0] * q_scr[0, pl.ds(g0, chunk), cols]
                    for cc in range(1, q_scr.shape[0]):
                        mixed = mixed + coef_ref[s, cc] * q_scr[cc, pl.ds(g0, chunk), cols]
                    pick = pick_ref[pl.ds(g0, chunk), pl.ds(s * records + r, 1)]
                    acc = acc + pick * mixed
                out_ref[pl.ds(g0 * cases + s, chunk, stride=cases), :] = acc
            return carry

        lax.fori_loop(0, groups // chunk, mix, 0)


def group_shares(case_coef, shape_groups, modal_resp, record_pick):
    comps, groups, modes = shape_groups.shape
    width = modal_resp.shape[1]
    cases = case_coef.shape[0]
    records = record_pick.shape[1] // cases
    steps = width // records
    return pl.pallas_call(
        functools.partial(mix_kernel, records=records),
        grid=(comps,),
        in_specs=[
            pl.BlockSpec(memory_space=pltpu.SMEM),
            pl.BlockSpec((1, groups, modes), lambda c: (c, 0, 0)),
            pl.BlockSpec((modes, width), lambda c: (0, 0)),
            pl.BlockSpec((groups, cases * records), lambda c: (0, 0)),
        ],
        out_specs=pl.BlockSpec((groups * cases, steps), lambda c: (0, 0)),
        out_shape=jax.ShapeDtypeStruct((groups * cases, steps), jnp.float32),
        scratch_shapes=[pltpu.VMEM((comps, groups, width), jnp.float32)],
        compiler_params=pltpu.CompilerParams(vmem_limit_bytes=48 * 1024 * 1024),
    )(case_coef, shape_groups, modal_resp, record_pick)


def local(
    ground_accel,
    modal_kernel,
    mode_shapes,
    member_owner,
    member_group,
    record_table,
    case_coef,
    gravity,
):
    tap_count = modal_kernel.shape[1]
    record_count = ground_accel.shape[0]
    comp_count = case_coef.shape[1]
    n_mode = lax.axis_size("mode")
    n_member = lax.axis_size("member")
    groups_here, case_count = gravity.shape
    owner_total = n_mode * n_member
    group_total = groups_here * owner_total
    group_index = member_owner[:, 0] * groups_here + member_group[:, 0]
    shape_groups = shape_sums(mode_shapes, group_index.reshape(1, -1), group_total, comp_count)
    lagged = lagged_table(ground_accel, tap_count)
    local_resp = lax.dot_general(
        modal_kernel[:, ::-1], lagged, (((1,), (1,)), ((), ())), preferred_element_type=jnp.float32
    ).astype(jnp.bfloat16)
    resp_rows, width = local_resp.shape
    rec_col = lax.all_to_all(
        jnp.broadcast_to(record_table[None], (n_mode,) + record_table.shape), "mode", 0, 0
    ).reshape(-1)
    rec_rows = -(-rec_col.shape[0] // width)
    rec_rows = -(-rec_rows // 8) * 8
    rec_block = jnp.zeros((rec_rows * width,), jnp.bfloat16).at[: rec_col.shape[0]].set(
        rec_col.astype(jnp.bfloat16)
    )
    payload = jnp.concatenate([local_resp, rec_block.reshape(rec_rows, width)], axis=0)
    gathered = lax.all_to_all(
        jnp.broadcast_to(payload[None], (n_member,) + payload.shape), "member", 0, 0
    )
    modal_resp = gathered[:, :resp_rows].reshape(n_member * resp_rows, width)
    rec_all = gathered[:, resp_rows:].reshape(n_member, -1)[:, : rec_col.shape[0]]
    rec_all = rec_all.astype(jnp.int32).reshape(n_member, n_mode, groups_here, case_count)
    rec_all = jnp.transpose(rec_all, (1, 0, 2, 3)).reshape(group_total, case_count)

    record_pick = (rec_all[:, :, None] == jnp.arange(record_count)[None, None, :]).astype(
        jnp.float32
    )
    share = group_shares(case_coef, shape_groups, modal_resp, record_pick.reshape(group_total, -1))
    share = share.reshape(owner_total, groups_here, case_count, share.shape[-1])
    received = lax.all_to_all(
        share.astype(jnp.bfloat16), ("mode", "member"), split_axis=0, concat_axis=0, tiled=True
    )
    selected = jnp.sum(received.astype(jnp.float32), axis=0)
    combined = gravity[:, :, None] + selected
    return jnp.max(jnp.abs(combined), axis=2)


def solution(mesh):
    placed = (
        P(),
        P(("mode", "member"), None),
        P("member", "mode"),
        P("member", None),
        P("member", None),
        P(("mode", "member"), None),
        P(),
        P(("mode", "member"), None),
    )
    return jax.shard_map(
        local, mesh=mesh, in_specs=placed, out_specs=P(("mode", "member"), None), check_vma=False
    )
```

```python
import functools

import jax
import jax.numpy as jnp
from jax import lax
from jax.experimental import pallas as pl
from jax.experimental.pallas import tpu as pltpu
from jax.sharding import PartitionSpec as P


def lagged_table(ground_accel, tap_count):
    record_count, span_len = ground_accel.shape
    step_count = span_len - tap_count + 1
    tiled = jnp.tile(ground_accel, (1, step_count + 1))[:, : step_count * (span_len + 1)]
    windows = tiled.reshape(record_count, step_count, span_len + 1)[:, :, :tap_count]
    return windows.reshape(record_count * step_count, tap_count)


def shape_sum_kernel(coef_ref, ms_ref, gi_ref, gs_ref, m_scr, g_scr, *, comps, tile):
    k = pl.program_id(0)
    rows = tile * comps
    slabs, _, lanes = m_scr.shape
    block = ms_ref[...].astype(jnp.float32)
    for l in range(slabs):
        m_scr[l, pl.ds(pl.multiple_of(k * rows, 8), rows), :] = block[:, l * lanes : (l + 1) * lanes]

    @pl.when(k == pl.num_programs(0) - 1)
    def _():
        groups = gs_ref.shape[1]
        members = gi_ref.shape[1]
        sel = (lax.broadcasted_iota(jnp.int32, (groups, members), 0) == gi_ref[...]).astype(
            jnp.bfloat16
        )
        for c in range(comps):
            comp_rows = jnp.concatenate(
                [m_scr[l, pl.ds(c, members, stride=comps), :] for l in range(slabs)], axis=1
            ).astype(jnp.bfloat16)
            g_scr[c] = jnp.dot(sel, comp_rows, preferred_element_type=jnp.float32)
        chunk = 64
        cases = gs_ref.shape[0]

        def mix(i, carry):
            g0 = pl.multiple_of(i * chunk, chunk)
            rows = pl.ds(g0, chunk)
            for s in range(cases):
                mixed = coef_ref[s, 0] * g_scr[0, rows, :]
                for c in range(1, comps):
                    mixed = mixed + coef_ref[s, c] * g_scr[c, rows, :]
                gs_ref[s, rows, :] = mixed.astype(jnp.bfloat16)
            return carry

        lax.fori_loop(0, groups // chunk, mix, 0)


def shape_sums(case_coef, mode_shapes, group_index, groups, tile=128):
    rows, modes = mode_shapes.shape
    cases, comps = case_coef.shape
    members = group_index.shape[1]
    return pl.pallas_call(
        functools.partial(shape_sum_kernel, comps=comps, tile=tile),
        grid=(members // tile,),
        in_specs=[
            pl.BlockSpec(memory_space=pltpu.SMEM),
            pl.BlockSpec((tile * comps, modes), lambda k: (k, 0)),
            pl.BlockSpec((1, members), lambda k: (0, 0)),
        ],
        out_specs=pl.BlockSpec((cases, groups, modes), lambda k: (0, 0, 0)),
        out_shape=jax.ShapeDtypeStruct((cases, groups, modes), jnp.bfloat16),
        scratch_shapes=[
            pltpu.VMEM((modes // 128, rows, 128), jnp.float32),
            pltpu.VMEM((comps, groups, modes), jnp.float32),
        ],
        compiler_params=pltpu.CompilerParams(vmem_limit_bytes=48 * 1024 * 1024),
    )(case_coef, mode_shapes, group_index)


def mix_kernel(gs_ref, resp_ref, pick_ref, out_ref, *, records):
    s = pl.program_id(0)
    cases = pl.num_programs(0)
    mixed = jnp.dot(gs_ref[0], resp_ref[...], preferred_element_type=jnp.float32)
    groups = mixed.shape[0]
    steps = mixed.shape[1] // records
    acc = None
    for r in range(records):
        pick = pick_ref[0, :, r : r + 1]
        term = pick * mixed[:, r * steps : (r + 1) * steps]
        acc = term if acc is None else acc + term
    out_ref[0] = acc


def group_shares(shape_groups, modal_resp, record_pick):
    cases, groups, modes = shape_groups.shape
    width = modal_resp.shape[1]
    records = record_pick.shape[2]
    steps = width // records
    return pl.pallas_call(
        functools.partial(mix_kernel, records=records),
        grid=(cases,),
        in_specs=[
            pl.BlockSpec((1, groups, modes), lambda s: (s, 0, 0)),
            pl.BlockSpec((modes, width), lambda s: (0, 0)),
            pl.BlockSpec((1, groups, records), lambda s: (s, 0, 0)),
        ],
        out_specs=pl.BlockSpec((1, groups, steps), lambda s: (s, 0, 0)),
        out_shape=jax.ShapeDtypeStruct((cases, groups, steps), jnp.float32),
        compiler_params=pltpu.CompilerParams(vmem_limit_bytes=48 * 1024 * 1024),
    )(shape_groups, modal_resp, record_pick)


def local(
    ground_accel,
    modal_kernel,
    mode_shapes,
    member_owner,
    member_group,
    record_table,
    case_coef,
    gravity,
):
    tap_count = modal_kernel.shape[1]
    record_count = ground_accel.shape[0]
    comp_count = case_coef.shape[1]
    n_mode = lax.axis_size("mode")
    n_member = lax.axis_size("member")
    groups_here, case_count = gravity.shape
    owner_total = n_mode * n_member
    group_total = groups_here * owner_total
    group_index = member_owner[:, 0] * groups_here + member_group[:, 0]
    shape_groups = shape_sums(case_coef, mode_shapes, group_index.reshape(1, -1), group_total)
    lagged = lagged_table(ground_accel, tap_count)
    local_resp = lax.dot_general(
        modal_kernel[:, ::-1], lagged, (((1,), (1,)), ((), ())), preferred_element_type=jnp.float32
    ).astype(jnp.bfloat16)
    resp_rows, width = local_resp.shape
    rec_col = lax.all_to_all(
        jnp.broadcast_to(record_table[None], (n_mode,) + record_table.shape), "mode", 0, 0
    ).reshape(-1)
    rec_rows = -(-rec_col.shape[0] // width)
    rec_rows = -(-rec_rows // 8) * 8
    rec_block = jnp.zeros((rec_rows * width,), jnp.bfloat16).at[: rec_col.shape[0]].set(
        rec_col.astype(jnp.bfloat16)
    )
    payload = jnp.concatenate([local_resp, rec_block.reshape(rec_rows, width)], axis=0)
    gathered = lax.all_to_all(
        jnp.broadcast_to(payload[None], (n_member,) + payload.shape), "member", 0, 0
    )
    modal_resp = gathered[:, :resp_rows].reshape(n_member * resp_rows, width)
    rec_all = gathered[:, resp_rows:].reshape(n_member, -1)[:, : rec_col.shape[0]]
    rec_all = rec_all.astype(jnp.int32).reshape(n_member, n_mode, groups_here, case_count)
    rec_all = jnp.transpose(rec_all, (1, 0, 2, 3)).reshape(group_total, case_count)

    record_pick = (rec_all.T[:, :, None] == jnp.arange(record_count)[None, None, :]).astype(
        jnp.float32
    )
    share = group_shares(shape_groups, modal_resp, record_pick)
    share = share.reshape(case_count, owner_total, groups_here, share.shape[-1])
    share = jnp.transpose(share.astype(jnp.bfloat16), (1, 2, 0, 3))
    received = lax.all_to_all(
        share, ("mode", "member"), split_axis=0, concat_axis=0, tiled=True
    )
    selected = jnp.sum(received.astype(jnp.float32), axis=0)
    combined = gravity[:, :, None] + selected
    return jnp.max(jnp.abs(combined), axis=2)


def solution(mesh):
    placed = (
        P(),
        P(("mode", "member"), None),
        P("member", "mode"),
        P("member", None),
        P("member", None),
        P(("mode", "member"), None),
        P(),
        P(("mode", "member"), None),
    )
    return jax.shard_map(
        local, mesh=mesh, in_specs=placed, out_specs=P(("mode", "member"), None), check_vma=False
    )
```

```python
import functools

import jax
import jax.numpy as jnp
from jax import lax
from jax.experimental import pallas as pl
from jax.experimental.pallas import tpu as pltpu
from jax.sharding import PartitionSpec as P


def lagged_table(ground_accel, tap_count):
    record_count, span_len = ground_accel.shape
    step_count = span_len - tap_count + 1
    tiled = jnp.tile(ground_accel, (1, step_count + 1))[:, : step_count * (span_len + 1)]
    windows = tiled.reshape(record_count, step_count, span_len + 1)[:, :, :tap_count]
    return windows.reshape(record_count * step_count, tap_count)


def shape_sum_kernel(ms_ref, gi_ref, gs_ref, m_scr, *, comps, tile):
    k = pl.program_id(0)
    rows = tile * comps
    slabs, _, lanes = m_scr.shape
    block = ms_ref[...].astype(jnp.float32)
    for l in range(slabs):
        m_scr[l, pl.ds(pl.multiple_of(k * rows, 8), rows), :] = block[:, l * lanes : (l + 1) * lanes]

    @pl.when(k == pl.num_programs(0) - 1)
    def _():
        groups = gs_ref.shape[1]
        members = gi_ref.shape[1]
        sel = (lax.broadcasted_iota(jnp.int32, (groups, members), 0) == gi_ref[...]).astype(
            jnp.bfloat16
        )
        for c in range(comps):
            comp_rows = jnp.concatenate(
                [m_scr[l, pl.ds(c, members, stride=comps), :] for l in range(slabs)], axis=1
            ).astype(jnp.bfloat16)
            gs_ref[c] = jnp.dot(sel, comp_rows, preferred_element_type=jnp.float32).astype(
                jnp.bfloat16
            )


def shape_sums(mode_shapes, group_index, groups, comps, tile=128):
    rows, modes = mode_shapes.shape
    members = group_index.shape[1]
    return pl.pallas_call(
        functools.partial(shape_sum_kernel, comps=comps, tile=tile),
        grid=(members // tile,),
        in_specs=[
            pl.BlockSpec((tile * comps, modes), lambda k: (k, 0)),
            pl.BlockSpec((1, members), lambda k: (0, 0)),
        ],
        out_specs=pl.BlockSpec((comps, groups, modes), lambda k: (0, 0, 0)),
        out_shape=jax.ShapeDtypeStruct((comps, groups, modes), jnp.bfloat16),
        scratch_shapes=[pltpu.VMEM((modes // 128, rows, 128), jnp.float32)],
        compiler_params=pltpu.CompilerParams(vmem_limit_bytes=48 * 1024 * 1024),
    )(mode_shapes, group_index)


def mix_kernel(coef_ref, gs_ref, g_ref, pick_ref, out_ref, q_scr, r_scr, *, records):
    c = pl.program_id(0)
    comps = pl.num_programs(0)
    senders, _, width = g_ref.shape
    resp_rows = r_scr.shape[0] // senders

    @pl.when(c == 0)
    def _():
        for j in range(senders):
            r_scr[pl.ds(j * resp_rows, resp_rows), :] = g_ref[j, pl.ds(0, resp_rows), :]

    q_scr[c] = jnp.dot(gs_ref[0], r_scr[...], preferred_element_type=jnp.float32)

    @pl.when(c == comps - 1)
    def _():
        groups = q_scr.shape[1]
        cases = coef_ref.shape[0]
        steps = q_scr.shape[2] // records
        chunk = 32

        def mix(i, carry):
            g0 = pl.multiple_of(i * chunk, chunk)
            rows = pl.ds(g0, chunk)
            accs = [jnp.zeros((chunk, steps), jnp.float32) for _ in range(cases)]
            for r in range(records):
                cols = pl.ds(r * steps, steps)
                slabs = [q_scr[cc, rows, cols] for cc in range(q_scr.shape[0])]
                for s in range(cases):
                    mixed = coef_ref[s, 0] * slabs[0]
                    for cc in range(1, len(slabs)):
                        mixed = mixed + coef_ref[s, cc] * slabs[cc]
                    accs[s] = accs[s] + pick_ref[rows, pl.ds(s * records + r, 1)] * mixed
            for s in range(cases):
                out_ref[pl.ds(g0 * cases + s, chunk, stride=cases), :] = accs[s]
            return carry

        lax.fori_loop(0, groups // chunk, mix, 0)


def group_shares(case_coef, shape_groups, gathered, resp_rows, record_pick):
    comps, groups, modes = shape_groups.shape
    width = gathered.shape[2]
    cases = case_coef.shape[0]
    records = record_pick.shape[1] // cases
    steps = width // records
    return pl.pallas_call(
        functools.partial(mix_kernel, records=records),
        grid=(comps,),
        in_specs=[
            pl.BlockSpec(memory_space=pltpu.SMEM),
            pl.BlockSpec((1, groups, modes), lambda c: (c, 0, 0)),
            pl.BlockSpec(gathered.shape, lambda c: (0, 0, 0)),
            pl.BlockSpec((groups, cases * records), lambda c: (0, 0)),
        ],
        out_specs=pl.BlockSpec((groups * cases, steps), lambda c: (0, 0)),
        out_shape=jax.ShapeDtypeStruct((groups * cases, steps), jnp.float32),
        scratch_shapes=[
            pltpu.VMEM((comps, groups, width), jnp.float32),
            pltpu.VMEM((modes, width), gathered.dtype),
        ],
        compiler_params=pltpu.CompilerParams(vmem_limit_bytes=48 * 1024 * 1024),
    )(case_coef, shape_groups, gathered, record_pick)


def local(
    ground_accel,
    modal_kernel,
    mode_shapes,
    member_owner,
    member_group,
    record_table,
    case_coef,
    gravity,
):
    tap_count = modal_kernel.shape[1]
    record_count = ground_accel.shape[0]
    comp_count = case_coef.shape[1]
    n_mode = lax.axis_size("mode")
    n_member = lax.axis_size("member")
    groups_here, case_count = gravity.shape
    owner_total = n_mode * n_member
    group_total = groups_here * owner_total
    group_index = member_owner[:, 0] * groups_here + member_group[:, 0]
    shape_groups = shape_sums(mode_shapes, group_index.reshape(1, -1), group_total, comp_count)
    lagged = lagged_table(ground_accel, tap_count)
    local_resp = lax.dot_general(
        modal_kernel[:, ::-1], lagged, (((1,), (1,)), ((), ())), preferred_element_type=jnp.float32
    ).astype(jnp.bfloat16)
    resp_rows, width = local_resp.shape
    rec_col = lax.all_to_all(
        jnp.broadcast_to(record_table[None], (n_mode,) + record_table.shape), "mode", 0, 0
    ).reshape(-1)
    rec_rows = -(-rec_col.shape[0] // width)
    rec_rows = -(-rec_rows // 8) * 8
    rec_block = jnp.zeros((rec_rows * width,), jnp.bfloat16).at[: rec_col.shape[0]].set(
        rec_col.astype(jnp.bfloat16)
    )
    payload = jnp.concatenate([local_resp, rec_block.reshape(rec_rows, width)], axis=0)
    gathered = lax.all_to_all(
        jnp.broadcast_to(payload[None], (n_member,) + payload.shape), "member", 0, 0
    )
    rec_all = gathered[:, resp_rows:].reshape(n_member, -1)[:, : rec_col.shape[0]]
    rec_all = rec_all.astype(jnp.int32).reshape(n_member, n_mode, groups_here, case_count)
    rec_all = jnp.transpose(rec_all, (1, 0, 2, 3)).reshape(group_total, case_count)

    record_pick = (rec_all[:, :, None] == jnp.arange(record_count)[None, None, :]).astype(
        jnp.float32
    )
    share = group_shares(
        case_coef, shape_groups, gathered, resp_rows, record_pick.reshape(group_total, -1)
    )
    share = share.reshape(owner_total, groups_here, case_count, share.shape[-1])
    received = lax.all_to_all(
        share.astype(jnp.bfloat16), ("mode", "member"), split_axis=0, concat_axis=0, tiled=True
    )
    selected = jnp.sum(received.astype(jnp.float32), axis=0)
    combined = gravity[:, :, None] + selected
    return jnp.max(jnp.abs(combined), axis=2)


def solution(mesh):
    placed = (
        P(),
        P(("mode", "member"), None),
        P("member", "mode"),
        P("member", None),
        P("member", None),
        P(("mode", "member"), None),
        P(),
        P(("mode", "member"), None),
    )
    return jax.shard_map(
        local, mesh=mesh, in_specs=placed, out_specs=P(("mode", "member"), None), check_vma=False
    )
```

```python
import functools

import jax
import jax.numpy as jnp
from jax import lax
from jax.experimental import pallas as pl
from jax.experimental.pallas import tpu as pltpu
from jax.sharding import PartitionSpec as P


def lagged_table(ground_accel, tap_count):
    record_count, span_len = ground_accel.shape
    step_count = span_len - tap_count + 1
    tiled = jnp.tile(ground_accel, (1, step_count + 1))[:, : step_count * (span_len + 1)]
    windows = tiled.reshape(record_count, step_count, span_len + 1)[:, :, :tap_count]
    return windows.reshape(record_count * step_count, tap_count)


def shape_sum_kernel(ms_ref, gi_ref, gs_ref, m_scr, *, comps, tile):
    k = pl.program_id(0)
    rows = tile * comps
    slabs, _, lanes = m_scr.shape
    block = ms_ref[...].astype(jnp.float32)
    for l in range(slabs):
        m_scr[l, pl.ds(pl.multiple_of(k * rows, 8), rows), :] = block[:, l * lanes : (l + 1) * lanes]

    @pl.when(k == pl.num_programs(0) - 1)
    def _():
        groups = gs_ref.shape[1]
        members = gi_ref.shape[1]
        sel = (lax.broadcasted_iota(jnp.int32, (groups, members), 0) == gi_ref[...]).astype(
            jnp.bfloat16
        )
        for c in range(comps):
            comp_rows = jnp.concatenate(
                [m_scr[l, pl.ds(c, members, stride=comps), :] for l in range(slabs)], axis=1
            ).astype(jnp.bfloat16)
            gs_ref[c] = jnp.dot(sel, comp_rows, preferred_element_type=jnp.float32).astype(
                jnp.bfloat16
            )


def shape_sums(mode_shapes, group_index, groups, comps, tile=128):
    rows, modes = mode_shapes.shape
    members = group_index.shape[1]
    return pl.pallas_call(
        functools.partial(shape_sum_kernel, comps=comps, tile=tile),
        grid=(members // tile,),
        in_specs=[
            pl.BlockSpec((tile * comps, modes), lambda k: (k, 0)),
            pl.BlockSpec((1, members), lambda k: (0, 0)),
        ],
        out_specs=pl.BlockSpec((comps, groups, modes), lambda k: (0, 0, 0)),
        out_shape=jax.ShapeDtypeStruct((comps, groups, modes), jnp.bfloat16),
        scratch_shapes=[pltpu.VMEM((modes // 128, rows, 128), jnp.float32)],
        compiler_params=pltpu.CompilerParams(vmem_limit_bytes=48 * 1024 * 1024),
    )(mode_shapes, group_index)


def mix_kernel(coef_ref, gs_ref, g_ref, pick_ref, out_ref, q_scr, r_scr, *, records):
    c = pl.program_id(0)
    comps = pl.num_programs(0)
    senders, _, width = g_ref.shape
    resp_rows = r_scr.shape[0] // senders

    @pl.when(c == 0)
    def _():
        for j in range(senders):
            r_scr[pl.ds(j * resp_rows, resp_rows), :] = g_ref[j, pl.ds(0, resp_rows), :]

    q_scr[...] = jnp.dot(gs_ref[0], r_scr[...], preferred_element_type=jnp.float32)
    groups = q_scr.shape[0]
    cases = coef_ref.shape[0]
    steps = q_scr.shape[1] // records
    chunk = 32

    def mix(i, carry):
        g0 = pl.multiple_of(i * chunk, chunk)
        rows = pl.ds(g0, chunk)
        for s in range(cases):
            picked = None
            for r in range(records):
                term = pick_ref[rows, pl.ds(s * records + r, 1)] * q_scr[rows, pl.ds(r * steps, steps)]
                picked = term if picked is None else picked + term
            dst = pl.ds(g0 * cases + s, chunk, stride=cases)
            term = coef_ref[s, c] * picked

            @pl.when(c == 0)
            def _():
                out_ref[dst, :] = term

            @pl.when(c > 0)
            def _():
                out_ref[dst, :] = out_ref[dst, :] + term

        return carry

    lax.fori_loop(0, groups // chunk, mix, 0)


def group_shares(case_coef, shape_groups, gathered, resp_rows, record_pick):
    comps, groups, modes = shape_groups.shape
    width = gathered.shape[2]
    cases = case_coef.shape[0]
    records = record_pick.shape[1] // cases
    steps = width // records
    return pl.pallas_call(
        functools.partial(mix_kernel, records=records),
        grid=(comps,),
        in_specs=[
            pl.BlockSpec(memory_space=pltpu.SMEM),
            pl.BlockSpec((1, groups, modes), lambda c: (c, 0, 0)),
            pl.BlockSpec(gathered.shape, lambda c: (0, 0, 0)),
            pl.BlockSpec((groups, cases * records), lambda c: (0, 0)),
        ],
        out_specs=pl.BlockSpec((groups * cases, steps), lambda c: (0, 0)),
        out_shape=jax.ShapeDtypeStruct((groups * cases, steps), jnp.float32),
        scratch_shapes=[
            pltpu.VMEM((groups, width), jnp.float32),
            pltpu.VMEM((modes, width), gathered.dtype),
        ],
        compiler_params=pltpu.CompilerParams(vmem_limit_bytes=48 * 1024 * 1024),
    )(case_coef, shape_groups, gathered, record_pick)


def local(
    ground_accel,
    modal_kernel,
    mode_shapes,
    member_owner,
    member_group,
    record_table,
    case_coef,
    gravity,
):
    tap_count = modal_kernel.shape[1]
    record_count = ground_accel.shape[0]
    comp_count = case_coef.shape[1]
    n_mode = lax.axis_size("mode")
    n_member = lax.axis_size("member")
    groups_here, case_count = gravity.shape
    owner_total = n_mode * n_member
    group_total = groups_here * owner_total
    group_index = member_owner[:, 0] * groups_here + member_group[:, 0]
    shape_groups = shape_sums(mode_shapes, group_index.reshape(1, -1), group_total, comp_count)
    lagged = lagged_table(ground_accel, tap_count)
    local_resp = lax.dot_general(
        modal_kernel[:, ::-1], lagged, (((1,), (1,)), ((), ())), preferred_element_type=jnp.float32
    ).astype(jnp.bfloat16)
    resp_rows, width = local_resp.shape
    rec_col = lax.all_to_all(
        jnp.broadcast_to(record_table[None], (n_mode,) + record_table.shape), "mode", 0, 0
    ).reshape(-1)
    rec_rows = -(-rec_col.shape[0] // width)
    rec_rows = -(-rec_rows // 8) * 8
    rec_block = jnp.zeros((rec_rows * width,), jnp.bfloat16).at[: rec_col.shape[0]].set(
        rec_col.astype(jnp.bfloat16)
    )
    payload = jnp.concatenate([local_resp, rec_block.reshape(rec_rows, width)], axis=0)
    gathered = lax.all_to_all(
        jnp.broadcast_to(payload[None], (n_member,) + payload.shape), "member", 0, 0
    )
    rec_all = gathered[:, resp_rows:].reshape(n_member, -1)[:, : rec_col.shape[0]]
    rec_all = rec_all.astype(jnp.int32).reshape(n_member, n_mode, groups_here, case_count)
    rec_all = jnp.transpose(rec_all, (1, 0, 2, 3)).reshape(group_total, case_count)

    record_pick = (rec_all[:, :, None] == jnp.arange(record_count)[None, None, :]).astype(
        jnp.float32
    )
    share = group_shares(
        case_coef, shape_groups, gathered, resp_rows, record_pick.reshape(group_total, -1)
    )
    share = share.reshape(owner_total, groups_here, case_count, share.shape[-1])
    received = lax.all_to_all(
        share.astype(jnp.bfloat16), ("mode", "member"), split_axis=0, concat_axis=0, tiled=True
    )
    selected = jnp.sum(received.astype(jnp.float32), axis=0)
    combined = gravity[:, :, None] + selected
    return jnp.max(jnp.abs(combined), axis=2)


def solution(mesh):
    placed = (
        P(),
        P(("mode", "member"), None),
        P("member", "mode"),
        P("member", None),
        P("member", None),
        P(("mode", "member"), None),
        P(),
        P(("mode", "member"), None),
    )
    return jax.shard_map(
        local, mesh=mesh, in_specs=placed, out_specs=P(("mode", "member"), None), check_vma=False
    )
```

```python
import functools

import jax
import jax.numpy as jnp
from jax import lax
from jax.experimental import pallas as pl
from jax.experimental.pallas import tpu as pltpu
from jax.sharding import PartitionSpec as P


def lagged_table(ground_accel, tap_count):
    record_count, span_len = ground_accel.shape
    step_count = span_len - tap_count + 1
    tiled = jnp.tile(ground_accel, (1, step_count + 1))[:, : step_count * (span_len + 1)]
    windows = tiled.reshape(record_count, step_count, span_len + 1)[:, :, :tap_count]
    return windows.reshape(record_count * step_count, tap_count)


def shape_sum_kernel(ms_ref, gi_ref, gs_ref, m_scr, *, comps, tile):
    k = pl.program_id(0)
    rows = tile * comps
    slabs, _, lanes = m_scr.shape
    block = ms_ref[...].astype(jnp.float32)
    for l in range(slabs):
        m_scr[l, pl.ds(pl.multiple_of(k * rows, 8), rows), :] = block[:, l * lanes : (l + 1) * lanes]

    @pl.when(k == pl.num_programs(0) - 1)
    def _():
        groups = gs_ref.shape[1]
        members = gi_ref.shape[1]
        sel = (lax.broadcasted_iota(jnp.int32, (groups, members), 0) == gi_ref[...]).astype(
            jnp.bfloat16
        )
        for c in range(comps):
            comp_rows = jnp.concatenate(
                [m_scr[l, pl.ds(c, members, stride=comps), :] for l in range(slabs)], axis=1
            ).astype(jnp.bfloat16)
            gs_ref[c] = jnp.dot(sel, comp_rows, preferred_element_type=jnp.float32).astype(
                jnp.bfloat16
            )


def shape_sums(mode_shapes, group_index, groups, comps, tile=128):
    rows, modes = mode_shapes.shape
    members = group_index.shape[1]
    return pl.pallas_call(
        functools.partial(shape_sum_kernel, comps=comps, tile=tile),
        grid=(members // tile,),
        in_specs=[
            pl.BlockSpec((tile * comps, modes), lambda k: (k, 0)),
            pl.BlockSpec((1, members), lambda k: (0, 0)),
        ],
        out_specs=pl.BlockSpec((comps, groups, modes), lambda k: (0, 0, 0)),
        out_shape=jax.ShapeDtypeStruct((comps, groups, modes), jnp.bfloat16),
        scratch_shapes=[pltpu.VMEM((modes // 128, rows, 128), jnp.float32)],
        compiler_params=pltpu.CompilerParams(vmem_limit_bytes=48 * 1024 * 1024),
    )(mode_shapes, group_index)


def mix_kernel(coef_ref, gs_ref, g_ref, pick_ref, out_ref, q_scr, r_scr, *, records):
    c = pl.program_id(0)
    comps = pl.num_programs(0)
    senders, _, width = g_ref.shape
    resp_rows = r_scr.shape[0] // senders

    @pl.when(c == 0)
    def _():
        for j in range(senders):
            r_scr[pl.ds(j * resp_rows, resp_rows), :] = g_ref[j, pl.ds(0, resp_rows), :]

    q_scr[c] = jnp.dot(gs_ref[0], r_scr[...], preferred_element_type=jnp.float32)

    @pl.when(c == comps - 1)
    def _():
        groups = q_scr.shape[1]
        cases = coef_ref.shape[0]
        steps = q_scr.shape[2] // records
        chunk = 64

        def mix(i, carry):
            g0 = pl.multiple_of(i * chunk, chunk)
            for s in range(cases):
                acc = jnp.zeros((chunk, steps), jnp.float32)
                for r in range(records):
                    cols = pl.ds(r * steps, steps)
                    mixed = coef_ref[s, 0] * q_scr[0, pl.ds(g0, chunk), cols]
                    for cc in range(1, q_scr.shape[0]):
                        mixed = mixed + coef_ref[s, cc] * q_scr[cc, pl.ds(g0, chunk), cols]
                    pick = pick_ref[pl.ds(g0, chunk), pl.ds(s * records + r, 1)]
                    acc = acc + pick * mixed
                out_ref[pl.ds(g0 * cases + s, chunk, stride=cases), :] = acc
            return carry

        lax.fori_loop(0, groups // chunk, mix, 0)


def group_shares(case_coef, shape_groups, gathered, resp_rows, record_pick):
    comps, groups, modes = shape_groups.shape
    width = gathered.shape[2]
    cases = case_coef.shape[0]
    records = record_pick.shape[1] // cases
    steps = width // records
    return pl.pallas_call(
        functools.partial(mix_kernel, records=records),
        grid=(comps,),
        in_specs=[
            pl.BlockSpec(memory_space=pltpu.SMEM),
            pl.BlockSpec((1, groups, modes), lambda c: (c, 0, 0)),
            pl.BlockSpec(gathered.shape, lambda c: (0, 0, 0)),
            pl.BlockSpec((groups, cases * records), lambda c: (0, 0)),
        ],
        out_specs=pl.BlockSpec((groups * cases, steps), lambda c: (0, 0)),
        out_shape=jax.ShapeDtypeStruct((groups * cases, steps), jnp.float32),
        scratch_shapes=[
            pltpu.VMEM((comps, groups, width), jnp.float32),
            pltpu.VMEM((modes, width), gathered.dtype),
        ],
        compiler_params=pltpu.CompilerParams(vmem_limit_bytes=48 * 1024 * 1024),
    )(case_coef, shape_groups, gathered, record_pick)


def local(
    ground_accel,
    modal_kernel,
    mode_shapes,
    member_owner,
    member_group,
    record_table,
    case_coef,
    gravity,
):
    tap_count = modal_kernel.shape[1]
    record_count = ground_accel.shape[0]
    comp_count = case_coef.shape[1]
    n_mode = lax.axis_size("mode")
    n_member = lax.axis_size("member")
    groups_here, case_count = gravity.shape
    owner_total = n_mode * n_member
    group_total = groups_here * owner_total
    group_index = member_owner[:, 0] * groups_here + member_group[:, 0]
    shape_groups = shape_sums(mode_shapes, group_index.reshape(1, -1), group_total, comp_count)
    lagged = lagged_table(ground_accel, tap_count)
    local_resp = lax.dot_general(
        modal_kernel[:, ::-1], lagged, (((1,), (1,)), ((), ())), preferred_element_type=jnp.float32
    ).astype(jnp.bfloat16)
    resp_rows, width = local_resp.shape
    rec_col = lax.all_to_all(
        jnp.broadcast_to(record_table[None], (n_mode,) + record_table.shape), "mode", 0, 0
    ).reshape(-1)
    rec_rows = -(-rec_col.shape[0] // width)
    rec_rows = -(-rec_rows // 8) * 8
    rec_block = jnp.zeros((rec_rows * width,), jnp.bfloat16).at[: rec_col.shape[0]].set(
        rec_col.astype(jnp.bfloat16)
    )
    payload = jnp.concatenate([local_resp, rec_block.reshape(rec_rows, width)], axis=0)
    gathered = lax.all_to_all(
        jnp.broadcast_to(payload[None], (n_member,) + payload.shape), "member", 0, 0
    )
    rec_all = gathered[:, resp_rows:].reshape(n_member, -1)[:, : rec_col.shape[0]]
    rec_all = rec_all.astype(jnp.int32).reshape(n_member, n_mode, groups_here, case_count)
    rec_all = jnp.transpose(rec_all, (1, 0, 2, 3)).reshape(group_total, case_count)

    record_pick = (rec_all[:, :, None] == jnp.arange(record_count)[None, None, :]).astype(
        jnp.float32
    )
    share = group_shares(
        case_coef, shape_groups, gathered, resp_rows, record_pick.reshape(group_total, -1)
    )
    share = share.reshape(owner_total, groups_here, case_count, share.shape[-1])
    received = lax.all_to_all(
        share.astype(jnp.bfloat16), ("mode", "member"), split_axis=0, concat_axis=0, tiled=True
    )
    selected = jnp.sum(received.astype(jnp.float32), axis=0)
    combined = gravity[:, :, None] + selected
    return jnp.max(jnp.abs(combined), axis=2)


def solution(mesh):
    placed = (
        P(),
        P(("mode", "member"), None),
        P("member", "mode"),
        P("member", None),
        P("member", None),
        P(("mode", "member"), None),
        P(),
        P(("mode", "member"), None),
    )
    return jax.shard_map(
        local, mesh=mesh, in_specs=placed, out_specs=P(("mode", "member"), None), check_vma=False
    )
```

```python
import functools

import jax
import jax.numpy as jnp
from jax import lax
from jax.experimental import pallas as pl
from jax.experimental.pallas import tpu as pltpu
from jax.sharding import PartitionSpec as P


def lagged_table(ground_accel, tap_count):
    record_count, span_len = ground_accel.shape
    step_count = span_len - tap_count + 1
    tiled = jnp.tile(ground_accel, (1, step_count + 1))[:, : step_count * (span_len + 1)]
    windows = tiled.reshape(record_count, step_count, span_len + 1)[:, :, :tap_count]
    return windows.reshape(record_count * step_count, tap_count)


def shape_sum_kernel(ms_ref, gi_ref, gs_ref, m_scr, *, comps, tile):
    k = pl.program_id(0)
    rows = tile * comps
    slabs, _, lanes = m_scr.shape
    block = ms_ref[...].astype(jnp.float32)
    for l in range(slabs):
        m_scr[l, pl.ds(pl.multiple_of(k * rows, 8), rows), :] = block[:, l * lanes : (l + 1) * lanes]

    @pl.when(k == pl.num_programs(0) - 1)
    def _():
        groups = gs_ref.shape[1]
        members = gi_ref.shape[1]
        sel = (lax.broadcasted_iota(jnp.int32, (groups, members), 0) == gi_ref[...]).astype(
            jnp.bfloat16
        )
        for c in range(comps):
            comp_rows = jnp.concatenate(
                [m_scr[l, pl.ds(c, members, stride=comps), :] for l in range(slabs)], axis=1
            ).astype(jnp.bfloat16)
            gs_ref[c] = jnp.dot(sel, comp_rows, preferred_element_type=jnp.float32).astype(
                jnp.bfloat16
            )


def shape_sums(mode_shapes, group_index, groups, comps, tile=128):
    rows, modes = mode_shapes.shape
    members = group_index.shape[1]
    return pl.pallas_call(
        functools.partial(shape_sum_kernel, comps=comps, tile=tile),
        grid=(members // tile,),
        in_specs=[
            pl.BlockSpec((tile * comps, modes), lambda k: (k, 0)),
            pl.BlockSpec((1, members), lambda k: (0, 0)),
        ],
        out_specs=pl.BlockSpec((comps, groups, modes), lambda k: (0, 0, 0)),
        out_shape=jax.ShapeDtypeStruct((comps, groups, modes), jnp.bfloat16),
        scratch_shapes=[pltpu.VMEM((modes // 128, rows, 128), jnp.float32)],
        compiler_params=pltpu.CompilerParams(vmem_limit_bytes=48 * 1024 * 1024),
    )(mode_shapes, group_index)


def mix_kernel(coef_ref, gs_ref, g_ref, rec_ref, out_ref, q_scr, r_scr, *, records, per_owner):
    c = pl.program_id(0)
    comps = pl.num_programs(0)
    senders, _, width = g_ref.shape
    resp_rows = r_scr.shape[0] // senders

    @pl.when(c == 0)
    def _():
        for j in range(senders):
            r_scr[pl.ds(j * resp_rows, resp_rows), :] = g_ref[j, pl.ds(0, resp_rows), :]

    q_scr[c] = jnp.dot(gs_ref[0], r_scr[...], preferred_element_type=jnp.float32)

    @pl.when(c == comps - 1)
    def _():
        groups = q_scr.shape[1]
        cases = coef_ref.shape[0]
        steps = q_scr.shape[2] // records
        slots = width // 128
        chunk = senders * per_owner
        for i in range(groups // chunk):
            g0 = i * chunk
            pick = jnp.concatenate(
                [
                    rec_ref[j, pl.ds(q * (rec_ref.shape[1] // per_owner) + i // slots, 1),
                            pl.ds((i % slots) * 128, 128)]
                    for j in range(senders)
                    for q in range(per_owner)
                ],
                axis=0,
            )
            for s in range(cases):
                acc = jnp.zeros((chunk, steps), jnp.float32)
                for r in range(records):
                    cols = pl.ds(r * steps, steps)
                    mixed = coef_ref[s, 0] * q_scr[0, pl.ds(g0, chunk), cols]
                    for cc in range(1, q_scr.shape[0]):
                        mixed = mixed + coef_ref[s, cc] * q_scr[cc, pl.ds(g0, chunk), cols]
                    acc = acc + pick[:, s * records + r : s * records + r + 1] * mixed
                out_ref[pl.ds(g0 * cases + s, chunk, stride=cases), :] = acc


def group_shares(case_coef, shape_groups, gathered, rec_rows, records, per_owner):
    comps, groups, modes = shape_groups.shape
    senders, _, width = gathered.shape
    cases = case_coef.shape[0]
    steps = width // records
    return pl.pallas_call(
        functools.partial(mix_kernel, records=records, per_owner=per_owner),
        grid=(comps,),
        in_specs=[
            pl.BlockSpec(memory_space=pltpu.SMEM),
            pl.BlockSpec((1, groups, modes), lambda c: (c, 0, 0)),
            pl.BlockSpec(gathered.shape, lambda c: (0, 0, 0)),
            pl.BlockSpec(rec_rows.shape, lambda c: (0, 0, 0)),
        ],
        out_specs=pl.BlockSpec((groups * cases, steps), lambda c: (0, 0)),
        out_shape=jax.ShapeDtypeStruct((groups * cases, steps), jnp.float32),
        scratch_shapes=[
            pltpu.VMEM((comps, groups, width), jnp.float32),
            pltpu.VMEM((modes, width), gathered.dtype),
        ],
        compiler_params=pltpu.CompilerParams(vmem_limit_bytes=48 * 1024 * 1024),
    )(case_coef, shape_groups, gathered, rec_rows)


def local(
    ground_accel,
    modal_kernel,
    mode_shapes,
    member_owner,
    member_group,
    record_table,
    case_coef,
    gravity,
):
    tap_count = modal_kernel.shape[1]
    record_count = ground_accel.shape[0]
    comp_count = case_coef.shape[1]
    n_mode = lax.axis_size("mode")
    n_member = lax.axis_size("member")
    groups_here, case_count = gravity.shape
    owner_total = n_mode * n_member
    group_total = groups_here * owner_total
    group_index = member_owner[:, 0] * groups_here + member_group[:, 0]
    shape_groups = shape_sums(mode_shapes, group_index.reshape(1, -1), group_total, comp_count)
    lagged = lagged_table(ground_accel, tap_count)
    local_resp = lax.dot_general(
        modal_kernel[:, ::-1], lagged, (((1,), (1,)), ((), ())), preferred_element_type=jnp.float32
    ).astype(jnp.bfloat16)
    resp_rows, width = local_resp.shape
    rec_col = lax.all_to_all(
        jnp.broadcast_to(record_table[None], (n_mode,) + record_table.shape), "mode", 0, 0
    ).reshape(-1)
    onehot = (rec_col.reshape(n_mode, groups_here, case_count)[..., None] == jnp.arange(record_count))
    onehot = onehot.reshape(n_mode, groups_here, case_count * record_count)
    onehot = jnp.pad(onehot, ((0, 0), (0, 0), (0, 128 - case_count * record_count)))
    rec_rows = groups_here * (n_mode * 128 // width)
    rec_block = jnp.transpose(onehot, (1, 0, 2)).reshape(rec_rows, width).astype(jnp.bfloat16)
    payload = jnp.concatenate([local_resp, rec_block], axis=0)
    gathered = lax.all_to_all(
        jnp.broadcast_to(payload[None], (n_member,) + payload.shape), "member", 0, 0
    )
    rec_rows_in = gathered[:, resp_rows:].astype(jnp.float32)
    share = group_shares(
        case_coef, shape_groups, gathered, rec_rows_in, record_count, groups_here
    )
    share = share.reshape(owner_total, groups_here, case_count, share.shape[-1])
    received = lax.all_to_all(
        share.astype(jnp.bfloat16), ("mode", "member"), split_axis=0, concat_axis=0, tiled=True
    )
    selected = jnp.sum(received.astype(jnp.float32), axis=0)
    combined = gravity[:, :, None] + selected
    return jnp.max(jnp.abs(combined), axis=2)


def solution(mesh):
    placed = (
        P(),
        P(("mode", "member"), None),
        P("member", "mode"),
        P("member", None),
        P("member", None),
        P(("mode", "member"), None),
        P(),
        P(("mode", "member"), None),
    )
    return jax.shard_map(
        local, mesh=mesh, in_specs=placed, out_specs=P(("mode", "member"), None), check_vma=False
    )
```

```python
import functools

import jax
import jax.numpy as jnp
from jax import lax
from jax.experimental import pallas as pl
from jax.experimental.pallas import tpu as pltpu
from jax.sharding import PartitionSpec as P


def lagged_table(ground_accel, tap_count):
    record_count, span_len = ground_accel.shape
    step_count = span_len - tap_count + 1
    tiled = jnp.tile(ground_accel, (1, step_count + 1))[:, : step_count * (span_len + 1)]
    windows = tiled.reshape(record_count, step_count, span_len + 1)[:, :, :tap_count]
    return windows.reshape(record_count * step_count, tap_count)


def shape_sum_kernel(ms_ref, gi_ref, gs_ref, m_scr, *, comps, tile):
    k = pl.program_id(0)
    rows = tile * comps
    slabs, _, lanes = m_scr.shape
    block = ms_ref[...].astype(jnp.float32)
    for l in range(slabs):
        m_scr[l, pl.ds(pl.multiple_of(k * rows, 8), rows), :] = block[:, l * lanes : (l + 1) * lanes]

    @pl.when(k == pl.num_programs(0) - 1)
    def _():
        groups = gs_ref.shape[1]
        members = gi_ref.shape[1]
        sel = (lax.broadcasted_iota(jnp.int32, (groups, members), 0) == gi_ref[...]).astype(
            jnp.bfloat16
        )
        for c in range(comps):
            comp_rows = jnp.concatenate(
                [m_scr[l, pl.ds(c, members, stride=comps), :] for l in range(slabs)], axis=1
            ).astype(jnp.bfloat16)
            gs_ref[c] = jnp.dot(sel, comp_rows, preferred_element_type=jnp.float32).astype(
                jnp.bfloat16
            )


def shape_sums(mode_shapes, group_index, groups, comps, tile=128):
    rows, modes = mode_shapes.shape
    members = group_index.shape[1]
    return pl.pallas_call(
        functools.partial(shape_sum_kernel, comps=comps, tile=tile),
        grid=(members // tile,),
        in_specs=[
            pl.BlockSpec((tile * comps, modes), lambda k: (k, 0)),
            pl.BlockSpec((1, members), lambda k: (0, 0)),
        ],
        out_specs=pl.BlockSpec((comps, groups, modes), lambda k: (0, 0, 0)),
        out_shape=jax.ShapeDtypeStruct((comps, groups, modes), jnp.bfloat16),
        scratch_shapes=[pltpu.VMEM((modes // 128, rows, 128), jnp.float32)],
        compiler_params=pltpu.CompilerParams(vmem_limit_bytes=48 * 1024 * 1024),
    )(mode_shapes, group_index)


def mix_kernel(
    coef_ref, gs_ref, g_ref, out_ref, q_scr, r_scr, *, records, per_owner, resp_rows, rec_rows
):
    c = pl.program_id(0)
    comps = pl.num_programs(0)
    senders, _, width = g_ref.shape

    @pl.when(c == 0)
    def _():
        for j in range(senders):
            r_scr[pl.ds(j * resp_rows, resp_rows), :] = g_ref[j, pl.ds(0, resp_rows), :]

    q_scr[c] = jnp.dot(gs_ref[0], r_scr[...], preferred_element_type=jnp.float32)

    @pl.when(c == comps - 1)
    def _():
        groups = q_scr.shape[1]
        cases = coef_ref.shape[0]
        steps = q_scr.shape[2] // records
        slots = width // 128
        chunk = senders * per_owner
        for i in range(groups // chunk):
            g0 = i * chunk
            pick = jnp.concatenate(
                [
                    g_ref[j, pl.ds(resp_rows + q * (rec_rows // per_owner) + i // slots, 1),
                          pl.ds((i % slots) * 128, 128)].astype(jnp.float32)
                    for j in range(senders)
                    for q in range(per_owner)
                ],
                axis=0,
            )
            for s in range(cases):
                acc = jnp.zeros((chunk, steps), jnp.float32)
                for r in range(records):
                    cols = pl.ds(r * steps, steps)
                    mixed = coef_ref[s, 0] * q_scr[0, pl.ds(g0, chunk), cols]
                    for cc in range(1, q_scr.shape[0]):
                        mixed = mixed + coef_ref[s, cc] * q_scr[cc, pl.ds(g0, chunk), cols]
                    acc = acc + pick[:, s * records + r : s * records + r + 1] * mixed
                out_ref[pl.ds(g0 * cases + s, chunk, stride=cases), :] = acc


def group_shares(case_coef, shape_groups, gathered, resp_rows, records, per_owner):
    comps, groups, modes = shape_groups.shape
    senders, _, width = gathered.shape
    cases = case_coef.shape[0]
    steps = width // records
    return pl.pallas_call(
        functools.partial(
            mix_kernel,
            records=records,
            per_owner=per_owner,
            resp_rows=resp_rows,
            rec_rows=gathered.shape[1] - resp_rows,
        ),
        grid=(comps,),
        in_specs=[
            pl.BlockSpec(memory_space=pltpu.SMEM),
            pl.BlockSpec((1, groups, modes), lambda c: (c, 0, 0)),
            pl.BlockSpec(gathered.shape, lambda c: (0, 0, 0)),
        ],
        out_specs=pl.BlockSpec((groups * cases, steps), lambda c: (0, 0)),
        out_shape=jax.ShapeDtypeStruct((groups * cases, steps), jnp.float32),
        scratch_shapes=[
            pltpu.VMEM((comps, groups, width), jnp.float32),
            pltpu.VMEM((modes, width), gathered.dtype),
        ],
        compiler_params=pltpu.CompilerParams(vmem_limit_bytes=48 * 1024 * 1024),
    )(case_coef, shape_groups, gathered)


def local(
    ground_accel,
    modal_kernel,
    mode_shapes,
    member_owner,
    member_group,
    record_table,
    case_coef,
    gravity,
):
    tap_count = modal_kernel.shape[1]
    record_count = ground_accel.shape[0]
    comp_count = case_coef.shape[1]
    n_mode = lax.axis_size("mode")
    n_member = lax.axis_size("member")
    groups_here, case_count = gravity.shape
    owner_total = n_mode * n_member
    group_total = groups_here * owner_total
    group_index = member_owner[:, 0] * groups_here + member_group[:, 0]
    shape_groups = shape_sums(mode_shapes, group_index.reshape(1, -1), group_total, comp_count)
    lagged = lagged_table(ground_accel, tap_count)
    local_resp = lax.dot_general(
        modal_kernel[:, ::-1], lagged, (((1,), (1,)), ((), ())), preferred_element_type=jnp.float32
    ).astype(jnp.bfloat16)
    resp_rows, width = local_resp.shape
    rec_col = lax.all_to_all(
        jnp.broadcast_to(record_table[None], (n_mode,) + record_table.shape), "mode", 0, 0
    ).reshape(-1)
    onehot = (rec_col.reshape(n_mode, groups_here, case_count)[..., None] == jnp.arange(record_count))
    onehot = onehot.reshape(n_mode, groups_here, case_count * record_count)
    onehot = jnp.pad(onehot, ((0, 0), (0, 0), (0, 128 - case_count * record_count)))
    rec_rows = groups_here * (n_mode * 128 // width)
    rec_block = jnp.transpose(onehot, (1, 0, 2)).reshape(rec_rows, width).astype(jnp.bfloat16)
    payload = jnp.concatenate([local_resp, rec_block], axis=0)
    gathered = lax.all_to_all(
        jnp.broadcast_to(payload[None], (n_member,) + payload.shape), "member", 0, 0
    )
    share = group_shares(
        case_coef, shape_groups, gathered, resp_rows, record_count, groups_here
    )
    share = share.reshape(owner_total, groups_here, case_count, share.shape[-1])
    received = lax.all_to_all(
        share.astype(jnp.bfloat16), ("mode", "member"), split_axis=0, concat_axis=0, tiled=True
    )
    selected = jnp.sum(received.astype(jnp.float32), axis=0)
    combined = gravity[:, :, None] + selected
    return jnp.max(jnp.abs(combined), axis=2)


def solution(mesh):
    placed = (
        P(),
        P(("mode", "member"), None),
        P("member", "mode"),
        P("member", None),
        P("member", None),
        P(("mode", "member"), None),
        P(),
        P(("mode", "member"), None),
    )
    return jax.shard_map(
        local, mesh=mesh, in_specs=placed, out_specs=P(("mode", "member"), None), check_vma=False
    )
```

```python
import functools

import jax
import jax.numpy as jnp
from jax import lax
from jax.experimental import pallas as pl
from jax.experimental.pallas import tpu as pltpu
from jax.sharding import PartitionSpec as P


def lagged_table(ground_accel, tap_count):
    record_count, span_len = ground_accel.shape
    step_count = span_len - tap_count + 1
    tiled = jnp.tile(ground_accel, (1, step_count + 1))[:, : step_count * (span_len + 1)]
    windows = tiled.reshape(record_count, step_count, span_len + 1)[:, :, :tap_count]
    return windows.reshape(record_count * step_count, tap_count)


def shape_sum_kernel(coef_ref, ms_ref, gi_ref, gs_ref, m_scr, g_scr, *, comps, tile):
    k = pl.program_id(0)
    rows = tile * comps
    slabs, _, lanes = m_scr.shape
    block = ms_ref[...].astype(jnp.float32)
    for l in range(slabs):
        m_scr[l, pl.ds(pl.multiple_of(k * rows, 8), rows), :] = block[:, l * lanes : (l + 1) * lanes]

    @pl.when(k == pl.num_programs(0) - 1)
    def _():
        groups = gs_ref.shape[1]
        members = gi_ref.shape[1]
        sel = (lax.broadcasted_iota(jnp.int32, (groups, members), 0) == gi_ref[...]).astype(
            jnp.bfloat16
        )
        for c in range(comps):
            comp_rows = jnp.concatenate(
                [m_scr[l, pl.ds(c, members, stride=comps), :] for l in range(slabs)], axis=1
            ).astype(jnp.bfloat16)
            g_scr[c] = jnp.dot(sel, comp_rows, preferred_element_type=jnp.float32)
        chunk = 64
        cases = gs_ref.shape[0]

        def mix(i, carry):
            g0 = pl.multiple_of(i * chunk, chunk)
            rows = pl.ds(g0, chunk)
            for s in range(cases):
                mixed = coef_ref[s, 0] * g_scr[0, rows, :]
                for c in range(1, comps):
                    mixed = mixed + coef_ref[s, c] * g_scr[c, rows, :]
                gs_ref[s, rows, :] = mixed.astype(jnp.bfloat16)
            return carry

        lax.fori_loop(0, groups // chunk, mix, 0)


def shape_sums(case_coef, mode_shapes, group_index, groups, tile=128):
    rows, modes = mode_shapes.shape
    cases, comps = case_coef.shape
    members = group_index.shape[1]
    return pl.pallas_call(
        functools.partial(shape_sum_kernel, comps=comps, tile=tile),
        grid=(members // tile,),
        in_specs=[
            pl.BlockSpec(memory_space=pltpu.SMEM),
            pl.BlockSpec((tile * comps, modes), lambda k: (k, 0)),
            pl.BlockSpec((1, members), lambda k: (0, 0)),
        ],
        out_specs=pl.BlockSpec((cases, groups, modes), lambda k: (0, 0, 0)),
        out_shape=jax.ShapeDtypeStruct((cases, groups, modes), jnp.bfloat16),
        scratch_shapes=[
            pltpu.VMEM((modes // 128, rows, 128), jnp.float32),
            pltpu.VMEM((comps, groups, modes), jnp.float32),
        ],
        compiler_params=pltpu.CompilerParams(vmem_limit_bytes=48 * 1024 * 1024),
    )(case_coef, mode_shapes, group_index)


def mix_kernel(gs_ref, g_ref, out_ref, r_scr, p_scr, *, records, per_owner, resp_rows, rec_rows):
    s = pl.program_id(0)
    cases = pl.num_programs(0)
    senders, _, width = g_ref.shape
    groups = p_scr.shape[0]
    slots = width // 128
    chunk = senders * per_owner

    @pl.when(s == 0)
    def _():
        for j in range(senders):
            r_scr[pl.ds(j * resp_rows, resp_rows), :] = g_ref[j, pl.ds(0, resp_rows), :]
        for i in range(groups // chunk):
            for j in range(senders):
                for q in range(per_owner):
                    row = resp_rows + q * (rec_rows // per_owner) + i // slots
                    p_scr[pl.ds(i * chunk + j * per_owner + q, 1), :] = g_ref[
                        j, pl.ds(row, 1), pl.ds((i % slots) * 128, 128)
                    ].astype(jnp.float32)

    mixed = jnp.dot(gs_ref[0], r_scr[...], preferred_element_type=jnp.float32)
    steps = mixed.shape[1] // records
    picked = None
    for r in range(records):
        col = p_scr[:, pl.ds(0, 128)]
        pick = jnp.sum(
            jnp.where(
                lax.broadcasted_iota(jnp.int32, col.shape, 1) == s * records + r, col, 0.0
            ),
            axis=1,
            keepdims=True,
        )
        term = pick * mixed[:, r * steps : (r + 1) * steps]
        picked = term if picked is None else picked + term
    out_ref[pl.ds(s, groups, stride=cases), :] = picked


def group_shares(shape_groups, gathered, resp_rows, records, per_owner):
    cases, groups, modes = shape_groups.shape
    senders, _, width = gathered.shape
    steps = width // records
    return pl.pallas_call(
        functools.partial(
            mix_kernel,
            records=records,
            per_owner=per_owner,
            resp_rows=resp_rows,
            rec_rows=gathered.shape[1] - resp_rows,
        ),
        grid=(cases,),
        in_specs=[
            pl.BlockSpec((1, groups, modes), lambda s: (s, 0, 0)),
            pl.BlockSpec(gathered.shape, lambda s: (0, 0, 0)),
        ],
        out_specs=pl.BlockSpec((groups * cases, steps), lambda s: (0, 0)),
        out_shape=jax.ShapeDtypeStruct((groups * cases, steps), jnp.float32),
        scratch_shapes=[
            pltpu.VMEM((modes, width), gathered.dtype),
            pltpu.VMEM((groups, 128), jnp.float32),
        ],
        compiler_params=pltpu.CompilerParams(vmem_limit_bytes=48 * 1024 * 1024),
    )(shape_groups, gathered)


def local(
    ground_accel,
    modal_kernel,
    mode_shapes,
    member_owner,
    member_group,
    record_table,
    case_coef,
    gravity,
):
    tap_count = modal_kernel.shape[1]
    record_count = ground_accel.shape[0]
    comp_count = case_coef.shape[1]
    n_mode = lax.axis_size("mode")
    n_member = lax.axis_size("member")
    groups_here, case_count = gravity.shape
    owner_total = n_mode * n_member
    group_total = groups_here * owner_total
    group_index = member_owner[:, 0] * groups_here + member_group[:, 0]
    shape_groups = shape_sums(case_coef, mode_shapes, group_index.reshape(1, -1), group_total)
    lagged = lagged_table(ground_accel, tap_count)
    local_resp = lax.dot_general(
        modal_kernel[:, ::-1], lagged, (((1,), (1,)), ((), ())), preferred_element_type=jnp.float32
    ).astype(jnp.bfloat16)
    resp_rows, width = local_resp.shape
    rec_col = lax.all_to_all(
        jnp.broadcast_to(record_table[None], (n_mode,) + record_table.shape), "mode", 0, 0
    ).reshape(-1)
    onehot = (rec_col.reshape(n_mode, groups_here, case_count)[..., None] == jnp.arange(record_count))
    onehot = onehot.reshape(n_mode, groups_here, case_count * record_count)
    onehot = jnp.pad(onehot, ((0, 0), (0, 0), (0, 128 - case_count * record_count)))
    rec_rows = groups_here * (n_mode * 128 // width)
    rec_block = jnp.transpose(onehot, (1, 0, 2)).reshape(rec_rows, width).astype(jnp.bfloat16)
    payload = jnp.concatenate([local_resp, rec_block], axis=0)
    gathered = lax.all_to_all(
        jnp.broadcast_to(payload[None], (n_member,) + payload.shape), "member", 0, 0
    )
    share = group_shares(shape_groups, gathered, resp_rows, record_count, groups_here)
    share = share.reshape(owner_total, groups_here, case_count, share.shape[-1])
    received = lax.all_to_all(
        share.astype(jnp.bfloat16), ("mode", "member"), split_axis=0, concat_axis=0, tiled=True
    )
    selected = jnp.sum(received.astype(jnp.float32), axis=0)
    combined = gravity[:, :, None] + selected
    return jnp.max(jnp.abs(combined), axis=2)


def solution(mesh):
    placed = (
        P(),
        P(("mode", "member"), None),
        P("member", "mode"),
        P("member", None),
        P("member", None),
        P(("mode", "member"), None),
        P(),
        P(("mode", "member"), None),
    )
    return jax.shard_map(
        local, mesh=mesh, in_specs=placed, out_specs=P(("mode", "member"), None), check_vma=False
    )
```

```python
import functools

import jax
import jax.numpy as jnp
from jax import lax
from jax.experimental import pallas as pl
from jax.experimental.pallas import tpu as pltpu
from jax.sharding import Mesh, PartitionSpec as P


def lagged_table(ground_accel, tap_count):
    record_count, span_len = ground_accel.shape
    step_count = span_len - tap_count + 1
    tiled = jnp.tile(ground_accel, (1, step_count + 1))[:, : step_count * (span_len + 1)]
    windows = tiled.reshape(record_count, step_count, span_len + 1)[:, :, :tap_count]
    return windows.reshape(record_count * step_count, tap_count)


def shape_sum_kernel(ms_ref, gi_ref, gs_ref, m_scr, *, comps, tile):
    k = pl.program_id(0)
    rows = tile * comps
    slabs, _, lanes = m_scr.shape
    block = ms_ref[...].astype(jnp.float32)
    for l in range(slabs):
        m_scr[l, pl.ds(pl.multiple_of(k * rows, 8), rows), :] = block[:, l * lanes : (l + 1) * lanes]

    @pl.when(k == pl.num_programs(0) - 1)
    def _():
        groups = gs_ref.shape[1]
        members = gi_ref.shape[1]
        sel = (lax.broadcasted_iota(jnp.int32, (groups, members), 0) == gi_ref[...]).astype(
            jnp.bfloat16
        )
        for c in range(comps):
            comp_rows = jnp.concatenate(
                [m_scr[l, pl.ds(c, members, stride=comps), :] for l in range(slabs)], axis=1
            ).astype(jnp.bfloat16)
            gs_ref[c] = jnp.dot(sel, comp_rows, preferred_element_type=jnp.float32).astype(
                jnp.bfloat16
            )


def shape_sums(mode_shapes, group_index, groups, comps, tile=128):
    rows, modes = mode_shapes.shape
    members = group_index.shape[1]
    return pl.pallas_call(
        functools.partial(shape_sum_kernel, comps=comps, tile=tile),
        grid=(members // tile,),
        in_specs=[
            pl.BlockSpec((tile * comps, modes), lambda k: (k, 0)),
            pl.BlockSpec((1, members), lambda k: (0, 0)),
        ],
        out_specs=pl.BlockSpec((comps, groups, modes), lambda k: (0, 0, 0)),
        out_shape=jax.ShapeDtypeStruct((comps, groups, modes), jnp.bfloat16),
        scratch_shapes=[pltpu.VMEM((modes // 128, rows, 128), jnp.float32)],
        compiler_params=pltpu.CompilerParams(vmem_limit_bytes=48 * 1024 * 1024),
    )(mode_shapes, group_index)


def mix_kernel(
    coef_ref, gs_ref, g_ref, out_ref, q_scr, r_scr, *, records, per_owner, resp_rows, rec_rows
):
    c = pl.program_id(0)
    comps = pl.num_programs(0)
    senders, _, width = g_ref.shape

    @pl.when(c == 0)
    def _():
        for j in range(senders):
            r_scr[pl.ds(j * resp_rows, resp_rows), :] = g_ref[j, pl.ds(0, resp_rows), :]

    q_scr[c] = jnp.dot(gs_ref[0], r_scr[...], preferred_element_type=jnp.float32)

    @pl.when(c == comps - 1)
    def _():
        groups = q_scr.shape[1]
        cases = coef_ref.shape[0]
        steps = q_scr.shape[2] // records
        slots = width // 128
        chunk = senders * per_owner
        for i in range(groups // chunk):
            g0 = i * chunk
            pick = jnp.concatenate(
                [
                    g_ref[j, pl.ds(resp_rows + q * (rec_rows // per_owner) + i // slots, 1),
                          pl.ds((i % slots) * 128, 128)].astype(jnp.float32)
                    for j in range(senders)
                    for q in range(per_owner)
                ],
                axis=0,
            )
            for s in range(cases):
                acc = jnp.zeros((chunk, steps), jnp.float32)
                for r in range(records):
                    cols = pl.ds(r * steps, steps)
                    mixed = coef_ref[s, 0] * q_scr[0, pl.ds(g0, chunk), cols]
                    for cc in range(1, q_scr.shape[0]):
                        mixed = mixed + coef_ref[s, cc] * q_scr[cc, pl.ds(g0, chunk), cols]
                    acc = acc + pick[:, s * records + r : s * records + r + 1] * mixed
                out_ref[pl.ds(g0 * cases + s, chunk, stride=cases), :] = acc


def group_shares(case_coef, shape_groups, gathered, resp_rows, records, per_owner):
    comps, groups, modes = shape_groups.shape
    senders, _, width = gathered.shape
    cases = case_coef.shape[0]
    steps = width // records
    return pl.pallas_call(
        functools.partial(
            mix_kernel,
            records=records,
            per_owner=per_owner,
            resp_rows=resp_rows,
            rec_rows=gathered.shape[1] - resp_rows,
        ),
        grid=(comps,),
        in_specs=[
            pl.BlockSpec(memory_space=pltpu.SMEM),
            pl.BlockSpec((1, groups, modes), lambda c: (c, 0, 0)),
            pl.BlockSpec(gathered.shape, lambda c: (0, 0, 0)),
        ],
        out_specs=pl.BlockSpec((groups * cases, steps), lambda c: (0, 0)),
        out_shape=jax.ShapeDtypeStruct((groups * cases, steps), jnp.float32),
        scratch_shapes=[
            pltpu.VMEM((comps, groups, width), jnp.float32),
            pltpu.VMEM((modes, width), gathered.dtype),
        ],
        compiler_params=pltpu.CompilerParams(vmem_limit_bytes=48 * 1024 * 1024),
    )(case_coef, shape_groups, gathered)


def local(
    ground_accel,
    modal_kernel,
    mode_shapes,
    member_owner,
    member_group,
    record_table,
    case_coef,
    gravity,
):
    tap_count = modal_kernel.shape[1]
    record_count = ground_accel.shape[0]
    comp_count = case_coef.shape[1]
    n_mode = lax.axis_size(MODE)
    n_member = lax.axis_size(MEMBER)
    groups_here, case_count = gravity.shape
    owner_total = n_mode * n_member
    group_total = groups_here * owner_total
    group_index = member_owner[:, 0] * groups_here + member_group[:, 0]
    shape_groups = shape_sums(mode_shapes, group_index.reshape(1, -1), group_total, comp_count)
    lagged = lagged_table(ground_accel, tap_count)
    local_resp = lax.dot_general(
        modal_kernel[:, ::-1], lagged, (((1,), (1,)), ((), ())), preferred_element_type=jnp.float32
    ).astype(jnp.bfloat16)
    resp_rows, width = local_resp.shape
    rec_col = lax.all_to_all(
        jnp.broadcast_to(record_table[None], (n_mode,) + record_table.shape), MODE, 0, 0
    ).reshape(-1)
    onehot = (rec_col.reshape(n_mode, groups_here, case_count)[..., None] == jnp.arange(record_count))
    onehot = onehot.reshape(n_mode, groups_here, case_count * record_count)
    onehot = jnp.pad(onehot, ((0, 0), (0, 0), (0, 128 - case_count * record_count)))
    rec_rows = groups_here * (n_mode * 128 // width)
    rec_block = jnp.transpose(onehot, (1, 0, 2)).reshape(rec_rows, width).astype(jnp.bfloat16)
    payload = jnp.concatenate([local_resp, rec_block], axis=0)
    inner = lax.axis_size(MEMBER[1])
    gathered = lax.all_to_all(
        jnp.broadcast_to(payload[None], (inner,) + payload.shape), MEMBER[1], 0, 0
    )
    gathered = lax.all_to_all(
        jnp.broadcast_to(gathered[None], (n_member // inner,) + gathered.shape), MEMBER[0], 0, 0
    ).reshape((n_member,) + payload.shape)
    share = group_shares(
        case_coef, shape_groups, gathered, resp_rows, record_count, groups_here
    )
    share = share.reshape(owner_total, groups_here, case_count, share.shape[-1])
    received = lax.all_to_all(
        share.astype(jnp.bfloat16), MODE + MEMBER, split_axis=0, concat_axis=0, tiled=True
    )
    selected = jnp.sum(received.astype(jnp.float32), axis=0)
    combined = gravity[:, :, None] + selected
    return jnp.max(jnp.abs(combined), axis=2)


MODE = ("x", "core")
MEMBER = ("z", "y")


def solution(mesh):
    n_mode, n_member = mesh.devices.shape
    outer = 2
    inner = 4
    fine = Mesh(
        mesh.devices.reshape(n_mode // outer, outer, n_member // inner, inner), MODE + MEMBER
    )
    every = MODE + MEMBER
    placed = (
        P(),
        P(every, None),
        P(MEMBER, MODE),
        P(MEMBER, None),
        P(MEMBER, None),
        P(every, None),
        P(),
        P(every, None),
    )
    return jax.shard_map(local, mesh=fine, in_specs=placed, out_specs=P(every, None), check_vma=False)
```

```python
import functools

import jax
import jax.numpy as jnp
from jax import lax
from jax.experimental import pallas as pl
from jax.experimental.pallas import tpu as pltpu
from jax.sharding import PartitionSpec as P


def lagged_table(ground_accel, tap_count):
    record_count, span_len = ground_accel.shape
    step_count = span_len - tap_count + 1
    tiled = jnp.tile(ground_accel, (1, step_count + 1))[:, : step_count * (span_len + 1)]
    windows = tiled.reshape(record_count, step_count, span_len + 1)[:, :, :tap_count]
    return windows.reshape(record_count * step_count, tap_count)


def shape_sum_kernel(ms_ref, gi_ref, gs_ref, m_scr, *, comps, tile):
    k = pl.program_id(0)
    rows = tile * comps
    slabs, _, lanes = m_scr.shape
    block = ms_ref[...].astype(jnp.float32)
    for l in range(slabs):
        m_scr[l, pl.ds(pl.multiple_of(k * rows, 8), rows), :] = block[:, l * lanes : (l + 1) * lanes]

    @pl.when(k == pl.num_programs(0) - 1)
    def _():
        groups = gs_ref.shape[1]
        members = gi_ref.shape[1]
        sel = (lax.broadcasted_iota(jnp.int32, (groups, members), 0) == gi_ref[...]).astype(
            jnp.bfloat16
        )
        for c in range(comps):
            comp_rows = jnp.concatenate(
                [m_scr[l, pl.ds(c, members, stride=comps), :] for l in range(slabs)], axis=1
            ).astype(jnp.bfloat16)
            gs_ref[c] = jnp.dot(sel, comp_rows, preferred_element_type=jnp.float32).astype(
                jnp.bfloat16
            )


def shape_sums(mode_shapes, group_index, groups, comps, tile=128):
    rows, modes = mode_shapes.shape
    members = group_index.shape[1]
    return pl.pallas_call(
        functools.partial(shape_sum_kernel, comps=comps, tile=tile),
        grid=(members // tile,),
        in_specs=[
            pl.BlockSpec((tile * comps, modes), lambda k: (k, 0)),
            pl.BlockSpec((1, members), lambda k: (0, 0)),
        ],
        out_specs=pl.BlockSpec((comps, groups, modes), lambda k: (0, 0, 0)),
        out_shape=jax.ShapeDtypeStruct((comps, groups, modes), jnp.bfloat16),
        scratch_shapes=[pltpu.VMEM((modes // 128, rows, 128), jnp.float32)],
        compiler_params=pltpu.CompilerParams(vmem_limit_bytes=48 * 1024 * 1024),
    )(mode_shapes, group_index)


def mix_kernel(
    coef_ref, gs_ref, g_ref, out_ref, q_scr, r_scr, *, records, per_owner, resp_rows, rec_rows
):
    c = pl.program_id(0)
    comps = pl.num_programs(0)
    senders, _, width = g_ref.shape

    @pl.when(c == 0)
    def _():
        for j in range(senders):
            r_scr[pl.ds(j * resp_rows, resp_rows), :] = g_ref[j, pl.ds(0, resp_rows), :]

    for e in range(gs_ref.shape[0]):
        q_scr[c * gs_ref.shape[0] + e] = jnp.dot(
            gs_ref[e], r_scr[...], preferred_element_type=jnp.float32
        )

    @pl.when(c == comps - 1)
    def _():
        groups = q_scr.shape[1]
        cases = coef_ref.shape[0]
        steps = q_scr.shape[2] // records
        slots = width // 128
        chunk = senders * per_owner
        for i in range(groups // chunk):
            g0 = i * chunk
            pick = jnp.concatenate(
                [
                    g_ref[j, pl.ds(resp_rows + q * (rec_rows // per_owner) + i // slots, 1),
                          pl.ds((i % slots) * 128, 128)].astype(jnp.float32)
                    for j in range(senders)
                    for q in range(per_owner)
                ],
                axis=0,
            )
            for s in range(cases):
                acc = jnp.zeros((chunk, steps), jnp.float32)
                for r in range(records):
                    cols = pl.ds(r * steps, steps)
                    mixed = coef_ref[s, 0] * q_scr[0, pl.ds(g0, chunk), cols]
                    for cc in range(1, q_scr.shape[0]):
                        mixed = mixed + coef_ref[s, cc] * q_scr[cc, pl.ds(g0, chunk), cols]
                    acc = acc + pick[:, s * records + r : s * records + r + 1] * mixed
                out_ref[pl.ds(g0 * cases + s, chunk, stride=cases), :] = acc


def group_shares(case_coef, shape_groups, gathered, resp_rows, records, per_owner):
    comps, groups, modes = shape_groups.shape
    senders, _, width = gathered.shape
    cases = case_coef.shape[0]
    steps = width // records
    return pl.pallas_call(
        functools.partial(
            mix_kernel,
            records=records,
            per_owner=per_owner,
            resp_rows=resp_rows,
            rec_rows=gathered.shape[1] - resp_rows,
        ),
        grid=(comps // 2,),
        in_specs=[
            pl.BlockSpec(memory_space=pltpu.SMEM),
            pl.BlockSpec((2, groups, modes), lambda c: (c, 0, 0)),
            pl.BlockSpec(gathered.shape, lambda c: (0, 0, 0)),
        ],
        out_specs=pl.BlockSpec((groups * cases, steps), lambda c: (0, 0)),
        out_shape=jax.ShapeDtypeStruct((groups * cases, steps), jnp.float32),
        scratch_shapes=[
            pltpu.VMEM((comps, groups, width), jnp.float32),
            pltpu.VMEM((modes, width), gathered.dtype),
        ],
        compiler_params=pltpu.CompilerParams(vmem_limit_bytes=48 * 1024 * 1024),
    )(case_coef, shape_groups, gathered)


def local(
    ground_accel,
    modal_kernel,
    mode_shapes,
    member_owner,
    member_group,
    record_table,
    case_coef,
    gravity,
):
    tap_count = modal_kernel.shape[1]
    record_count = ground_accel.shape[0]
    comp_count = case_coef.shape[1]
    n_mode = lax.axis_size("mode")
    n_member = lax.axis_size("member")
    groups_here, case_count = gravity.shape
    owner_total = n_mode * n_member
    group_total = groups_here * owner_total
    group_index = member_owner[:, 0] * groups_here + member_group[:, 0]
    shape_groups = shape_sums(mode_shapes, group_index.reshape(1, -1), group_total, comp_count)
    lagged = lagged_table(ground_accel, tap_count)
    local_resp = lax.dot_general(
        modal_kernel[:, ::-1], lagged, (((1,), (1,)), ((), ())), preferred_element_type=jnp.float32
    ).astype(jnp.bfloat16)
    resp_rows, width = local_resp.shape
    rec_col = lax.all_to_all(
        jnp.broadcast_to(record_table[None], (n_mode,) + record_table.shape), "mode", 0, 0
    ).reshape(-1)
    onehot = (rec_col.reshape(n_mode, groups_here, case_count)[..., None] == jnp.arange(record_count))
    onehot = onehot.reshape(n_mode, groups_here, case_count * record_count)
    onehot = jnp.pad(onehot, ((0, 0), (0, 0), (0, 128 - case_count * record_count)))
    rec_rows = groups_here * (n_mode * 128 // width)
    rec_block = jnp.transpose(onehot, (1, 0, 2)).reshape(rec_rows, width).astype(jnp.bfloat16)
    payload = jnp.concatenate([local_resp, rec_block], axis=0)
    gathered = lax.all_to_all(
        jnp.broadcast_to(payload[None], (n_member,) + payload.shape), "member", 0, 0
    )
    share = group_shares(
        case_coef, shape_groups, gathered, resp_rows, record_count, groups_here
    )
    share = share.reshape(owner_total, groups_here, case_count, share.shape[-1])
    received = lax.all_to_all(
        share.astype(jnp.bfloat16), ("mode", "member"), split_axis=0, concat_axis=0, tiled=True
    )
    selected = jnp.sum(received.astype(jnp.float32), axis=0)
    combined = gravity[:, :, None] + selected
    return jnp.max(jnp.abs(combined), axis=2)


def solution(mesh):
    placed = (
        P(),
        P(("mode", "member"), None),
        P("member", "mode"),
        P("member", None),
        P("member", None),
        P(("mode", "member"), None),
        P(),
        P(("mode", "member"), None),
    )
    return jax.shard_map(
        local, mesh=mesh, in_specs=placed, out_specs=P(("mode", "member"), None), check_vma=False
    )
```

```python
import functools

import jax
import jax.numpy as jnp
from jax import lax
from jax.experimental import pallas as pl
from jax.experimental.pallas import tpu as pltpu
from jax.sharding import PartitionSpec as P


def lagged_table(ground_accel, tap_count):
    record_count, span_len = ground_accel.shape
    step_count = span_len - tap_count + 1
    tiled = jnp.tile(ground_accel, (1, step_count + 1))[:, : step_count * (span_len + 1)]
    windows = tiled.reshape(record_count, step_count, span_len + 1)[:, :, :tap_count]
    return windows.reshape(record_count * step_count, tap_count)


def shape_sum_kernel(ms_ref, gi_ref, gs_ref, m_scr, *, comps, tile):
    k = pl.program_id(0)
    rows = tile * comps
    slabs, _, lanes = m_scr.shape
    block = ms_ref[...].astype(jnp.float32)
    for l in range(slabs):
        m_scr[l, pl.ds(pl.multiple_of(k * rows, 8), rows), :] = block[:, l * lanes : (l + 1) * lanes]

    @pl.when(k == pl.num_programs(0) - 1)
    def _():
        groups = gs_ref.shape[1]
        members = gi_ref.shape[1]
        sel = (lax.broadcasted_iota(jnp.int32, (groups, members), 0) == gi_ref[...]).astype(
            jnp.bfloat16
        )
        for c in range(comps):
            comp_rows = jnp.concatenate(
                [m_scr[l, pl.ds(c, members, stride=comps), :] for l in range(slabs)], axis=1
            ).astype(jnp.bfloat16)
            gs_ref[c] = jnp.dot(sel, comp_rows, preferred_element_type=jnp.float32).astype(
                jnp.bfloat16
            )


def shape_sums(mode_shapes, group_index, groups, comps, tile=128):
    rows, modes = mode_shapes.shape
    members = group_index.shape[1]
    return pl.pallas_call(
        functools.partial(shape_sum_kernel, comps=comps, tile=tile),
        grid=(members // tile,),
        in_specs=[
            pl.BlockSpec((tile * comps, modes), lambda k: (k, 0)),
            pl.BlockSpec((1, members), lambda k: (0, 0)),
        ],
        out_specs=pl.BlockSpec((comps, groups, modes), lambda k: (0, 0, 0)),
        out_shape=jax.ShapeDtypeStruct((comps, groups, modes), jnp.bfloat16),
        scratch_shapes=[pltpu.VMEM((modes // 128, rows, 128), jnp.float32)],
        compiler_params=pltpu.CompilerParams(vmem_limit_bytes=48 * 1024 * 1024),
    )(mode_shapes, group_index)


def mix_kernel(
    coef_ref, gs_ref, g_ref, out_ref, q_scr, r_scr, *, records, per_owner, resp_rows, rec_rows
):
    c = pl.program_id(0)
    comps = pl.num_programs(0)
    senders, _, width = g_ref.shape

    @pl.when(c == 0)
    def _():
        for j in range(senders):
            r_scr[pl.ds(j * resp_rows, resp_rows), :] = g_ref[j, pl.ds(0, resp_rows), :]

    for e in range(gs_ref.shape[0]):
        q_scr[c * gs_ref.shape[0] + e] = jnp.dot(
            gs_ref[e], r_scr[...], preferred_element_type=jnp.float32
        )

    @pl.when(c == comps - 1)
    def _():
        groups = q_scr.shape[1]
        cases = coef_ref.shape[0]
        steps = q_scr.shape[2] // records
        slots = width // 128
        chunk = senders * per_owner
        for i in range(groups // chunk):
            g0 = i * chunk
            pick = jnp.concatenate(
                [
                    g_ref[j, pl.ds(resp_rows + q * (rec_rows // per_owner) + i // slots, 1),
                          pl.ds((i % slots) * 128, 128)].astype(jnp.float32)
                    for j in range(senders)
                    for q in range(per_owner)
                ],
                axis=0,
            )
            for s in range(cases):
                acc = jnp.zeros((chunk, steps), jnp.float32)
                for r in range(records):
                    cols = pl.ds(r * steps, steps)
                    mixed = coef_ref[s, 0] * q_scr[0, pl.ds(g0, chunk), cols]
                    for cc in range(1, q_scr.shape[0]):
                        mixed = mixed + coef_ref[s, cc] * q_scr[cc, pl.ds(g0, chunk), cols]
                    acc = acc + pick[:, s * records + r : s * records + r + 1] * mixed
                out_ref[pl.ds(g0 * cases + s, chunk, stride=cases), :] = acc


def group_shares(case_coef, shape_groups, gathered, resp_rows, records, per_owner):
    comps, groups, modes = shape_groups.shape
    senders, _, width = gathered.shape
    cases = case_coef.shape[0]
    steps = width // records
    return pl.pallas_call(
        functools.partial(
            mix_kernel,
            records=records,
            per_owner=per_owner,
            resp_rows=resp_rows,
            rec_rows=gathered.shape[1] - resp_rows,
        ),
        grid=(comps // 3,),
        in_specs=[
            pl.BlockSpec(memory_space=pltpu.SMEM),
            pl.BlockSpec((3, groups, modes), lambda c: (c, 0, 0)),
            pl.BlockSpec(gathered.shape, lambda c: (0, 0, 0)),
        ],
        out_specs=pl.BlockSpec((groups * cases, steps), lambda c: (0, 0)),
        out_shape=jax.ShapeDtypeStruct((groups * cases, steps), jnp.float32),
        scratch_shapes=[
            pltpu.VMEM((comps, groups, width), jnp.float32),
            pltpu.VMEM((modes, width), gathered.dtype),
        ],
        compiler_params=pltpu.CompilerParams(vmem_limit_bytes=48 * 1024 * 1024),
    )(case_coef, shape_groups, gathered)


def local(
    ground_accel,
    modal_kernel,
    mode_shapes,
    member_owner,
    member_group,
    record_table,
    case_coef,
    gravity,
):
    tap_count = modal_kernel.shape[1]
    record_count = ground_accel.shape[0]
    comp_count = case_coef.shape[1]
    n_mode = lax.axis_size("mode")
    n_member = lax.axis_size("member")
    groups_here, case_count = gravity.shape
    owner_total = n_mode * n_member
    group_total = groups_here * owner_total
    group_index = member_owner[:, 0] * groups_here + member_group[:, 0]
    shape_groups = shape_sums(mode_shapes, group_index.reshape(1, -1), group_total, comp_count)
    lagged = lagged_table(ground_accel, tap_count)
    local_resp = lax.dot_general(
        modal_kernel[:, ::-1], lagged, (((1,), (1,)), ((), ())), preferred_element_type=jnp.float32
    ).astype(jnp.bfloat16)
    resp_rows, width = local_resp.shape
    rec_col = lax.all_to_all(
        jnp.broadcast_to(record_table[None], (n_mode,) + record_table.shape), "mode", 0, 0
    ).reshape(-1)
    onehot = (rec_col.reshape(n_mode, groups_here, case_count)[..., None] == jnp.arange(record_count))
    onehot = onehot.reshape(n_mode, groups_here, case_count * record_count)
    onehot = jnp.pad(onehot, ((0, 0), (0, 0), (0, 128 - case_count * record_count)))
    rec_rows = groups_here * (n_mode * 128 // width)
    rec_block = jnp.transpose(onehot, (1, 0, 2)).reshape(rec_rows, width).astype(jnp.bfloat16)
    payload = jnp.concatenate([local_resp, rec_block], axis=0)
    gathered = lax.all_to_all(
        jnp.broadcast_to(payload[None], (n_member,) + payload.shape), "member", 0, 0
    )
    share = group_shares(
        case_coef, shape_groups, gathered, resp_rows, record_count, groups_here
    )
    share = share.reshape(owner_total, groups_here, case_count, share.shape[-1])
    received = lax.all_to_all(
        share.astype(jnp.bfloat16), ("mode", "member"), split_axis=0, concat_axis=0, tiled=True
    )
    selected = jnp.sum(received.astype(jnp.float32), axis=0)
    combined = gravity[:, :, None] + selected
    return jnp.max(jnp.abs(combined), axis=2)


def solution(mesh):
    placed = (
        P(),
        P(("mode", "member"), None),
        P("member", "mode"),
        P("member", None),
        P("member", None),
        P(("mode", "member"), None),
        P(),
        P(("mode", "member"), None),
    )
    return jax.shard_map(
        local, mesh=mesh, in_specs=placed, out_specs=P(("mode", "member"), None), check_vma=False
    )
```
